256 devices in a mesh: stream: 8 (over z), span: 32 (over y, x, core).
Axes of the slice: x: 4, y: 4, z: 8, core: 2. Of those that a mesh axis runs over, the one named last changes fastest.
Arguments:
- velocity: float32 [3, 64, 512, 1024], P(None, 'stream', 'span'), may hold values from -36 to 36
- coefficient: float32 [64, 512, 1024], P('stream', 'span'), may hold values from 0.5 to 4
- coords: float32 [3, 32768], P(None, ('stream', 'span')), may hold values from -1 to 1
- forces: float32 [3, 32768], P(None, ('stream', 'span')), may hold values from -12 to 12
- line_id: int32 [32768], P(('stream', 'span')), may hold values from 0 to 399
- line_gain: float32 [400], replicated, may hold values from 0.5 to 2
- dest_span: int32 [32768, 1], P(('stream', 'span')), may hold values from 0 to 31; in each aligned block of 128 rows (0 to 127, 128 to 255, ...) at most 8 rows name the same one
- owner_element: int32 [32768], P(('stream', 'span')), may hold values from 0 to 255
Outputs:
- pressure: float32 [64, 512, 1024], P('stream', 'span')
- residual: float32 [64, 512, 1024], P('stream', 'span')
The draws below stay inside these ranges and needn't reach their ends.
Inputs may be any that keep to these rules, and one draw needn't show every extreme that they name: `dest_span`: of the 128 blade points of one device, at most 8 name the same span index, and in every draw some span index is named by exactly 8 of one device's points. `owner_element`: an element of the device at the point's span index in the same slab, numbered (ex * 2 + ey) * 128 + ez.
All inputs are finite; a program needn't handle non-finite values.
Results may differ from the reference program's by a relative error of at most 0.00019.
Values sent between devices are 32-bit elements; how exact they have to be, the bound alone decides.
No kernel may reach another device: no remote copies, remote signals or barrier semaphores. Data moves between devices by JAX's collectives and lax.ppermute only.
A program may use at most 64 MiB of HBM per device.

```python
import math
import jax
import jax.numpy as jnp
import numpy as np
from jax import lax

POLY = 8
EX = 1
EY = 2
EZ = 128
PTS_DEV = 128
LINES = 400
ITERS = 3
CAP = 8
SLAB_PTS = 4096
POINTS = 32768
GX = 64
GY = 512
GZ = 1024
N_SPAN = 32


def draw_velocity(key, part):
    stream_frac = jnp.arange(GX, dtype=jnp.float32) / GX
    span_frac = jnp.arange(GY, dtype=jnp.float32) / GY
    amplitude = 0.3 * (1.0 + 2.0 * stream_frac)[:, None] * (10.0 ** span_frac)[None, :]
    noise_field = jnp.clip(jax.random.normal(key, (3, GX, GY, GZ), jnp.float32), -4.0, 4.0)
    return noise_field * amplitude[None, :, :, None]


def with_ends(array, stream_key, least, top_value):
    shape = array.shape
    index_at = [jax.random.randint(jax.random.fold_in(stream_key, axis), (), 0, shape[axis]) for axis in range(len(shape))]
    array = array.at[tuple(index_at)].set(least)
    longest = shape.index(max(shape))
    index_at[longest] = (index_at[longest] + 1) % shape[longest]
    return array.at[tuple(index_at)].set(top_value)


def block_scale(own_key, dims, cuts, low, top_value):
    gain, own = 1.0, jax.random.fold_in(own_key, 6)
    for dim, parts in cuts:
        draws = jnp.exp(jax.random.uniform(jax.random.fold_in(own, dim), (parts,), jnp.float32, low / len(cuts), top_value / len(cuts)))
        gain = gain * jnp.repeat(draws, dims[dim] // parts).reshape([-1 if axis == dim else 1 for axis in range(len(dims))])
    return gain


def routed_block(stream_key, own, number, rows, amount, top, limit, skew):
    order = jax.random.permutation(stream_key, amount)
    crowded, usual = load_shares(amount, rows * top, limit, skew, True), load_shares(amount, rows * top, limit, skew, False)
    places = jnp.arange(amount)

    def named(lengths, offset_by):
        used = int((lengths > 0).sum())
        fixed = max(1, used // 4)
        moved = fixed + (places - fixed + offset_by * (used - fixed)) % max(1, amount - fixed)
        return jnp.zeros((amount,), jnp.int32).at[order[jnp.where(places < fixed, places, moved)]].set(jnp.asarray(lengths, jnp.int32))

    lengths = jnp.where(number % 4 == 0, named(crowded, number // 4), named(usual, number - number // 4 - 1))
    mixed = jax.random.permutation(jax.random.fold_in(own, 3), amount)
    giver, sink = mixed[0:amount // 2 * 2:2], mixed[1:amount // 2 * 2:2]
    margin = jnp.minimum(lengths[giver] - 1, limit - lengths[sink]) // 2
    margin = jnp.where((giver == order[0]) | (sink == order[0]) | (lengths[sink] == 0), 0, jnp.maximum(margin, 0))
    moved = jax.random.randint(jax.random.fold_in(own, 4), (amount // 2,), 0, 1 << 20) % (margin + 1)
    lengths = lengths.at[giver].add(-moved).at[sink].add(moved)
    items = jnp.searchsorted(jnp.cumsum(lengths), jnp.arange(rows * top), side="right").astype(jnp.int32)
    table = items.reshape(top, rows).T
    table = table[jax.random.permutation(jax.random.fold_in(own, 1), rows)]
    offset_by = jax.random.randint(jax.random.fold_in(own, 2), (rows, 1), 0, top)
    return jnp.take_along_axis(table, (jnp.arange(top)[None, :] + offset_by) % top, axis=1)


def load_shares(number_of, total, most, slope, full):
    weights = [(1 << 20) // math.isqrt(standing ** slope) + 1 for standing in range(1, number_of + 1)]
    largest = most if full else min(most, max(-(-total // number_of), total * weights[0] // sum(weights)))
    least = 1 if total - largest >= number_of - 1 else 0
    holding, spare = [largest] + [least] * (number_of - 1), total - largest - least * (number_of - 1)
    while spare > 0:
        free = [i for i in range(1, number_of) if holding[i] < largest] or [i for i in range(1, number_of) if holding[i] < most]
        mass, remaining = sum([weights[i] for i in free]), spare
        for i in free:
            more = min(most - holding[i], max(1, remaining * weights[i] // mass), spare)
            holding[i] = holding[i] + more
            spare = spare - more
    return np.array(holding)


def noise(stream_key, shape, deviation, most, cuts=(), kind=jnp.bfloat16):
    level = block_scale(stream_key, shape, cuts, -0.22, 0.18) if cuts else 1.0
    values = jax.random.normal(stream_key, shape, jnp.float32) * deviation * level
    return jnp.minimum(jnp.maximum(values, -most), most).astype(kind)


def setup_inputs(seed: int = 0) -> dict:
    splits = jax.random.split(jax.random.key(seed), 9)
    velocity = draw_velocity(jax.random.fold_in(splits[8], 71), 0)
    coefficient = jnp.clip(jnp.exp(math.log(4.0) - 2.0794415 * jax.random.uniform(splits[1], (GX, GY, GZ), jnp.float32) ** block_scale(splits[1], (GX, GY, GZ), ((0, 8), (1, 32)), -0.2, 0.2)), 0.5, 4.0)
    coords = jnp.clip(jax.random.uniform(splits[2], (3, POINTS), jnp.float32, -1.0, 1.0) * block_scale(splits[2], (3, POINTS), ((1, 256),), -0.4, 0.0), -1.0, 1.0)
    forces = noise(splits[3], (3, POINTS), 3.0, 12.0, ((1, 256),), jnp.float32)
    line_id = with_ends(jax.random.randint(splits[4], (POINTS,), 0, LINES), jax.random.fold_in(splits[4], 1), 0, LINES - 1).astype(jnp.int32)
    line_gain = jnp.clip(jnp.exp(jax.random.uniform(splits[5], (LINES,), jnp.float32, math.log(0.5), math.log(2.0))), 0.5, 2.0)
    dest_span_keys = jax.random.split(jax.random.fold_in(splits[6], 1), POINTS // PTS_DEV)
    dest_span_turns = jax.random.permutation(jax.random.fold_in(splits[6], 3), POINTS // PTS_DEV)
    dest_span = jax.vmap(lambda own, number: routed_block(jax.random.fold_in(splits[6], 2), own, number, PTS_DEV, N_SPAN, 1, CAP, 2))(dest_span_keys, dest_span_turns).reshape((POINTS, 1))
    owner_element = with_ends(jax.random.randint(splits[7], (POINTS,), 0, EX * EY * EZ), jax.random.fold_in(splits[7], 1), 0, (EX * EY * EZ) - 1).astype(jnp.int32)
    return {"velocity": velocity, "coefficient": coefficient, "coords": coords, "forces": forces, "line_id": line_id, "line_gain": line_gain, "dest_span": dest_span, "owner_element": owner_element}


kernel_width = 0.45
gll_nodes = [-1.0, -0.8717401485096066, -0.5917001814331423, -0.2092992179024789,
             0.2092992179024789, 0.5917001814331423, 0.8717401485096066, 1.0]


def legendre_value(point, degree):
    previous = 1.0
    current = point
    for order in range(1, degree):
        following = ((2 * order + 1) * point * current - order * previous) / (order + 1)
        previous = current
        current = following
    return current


def gll_tables():
    degree = POLY - 1
    values = [legendre_value(point, degree) for point in gll_nodes]
    weights = [2.0 / (degree * (degree + 1) * value * value) for value in values]
    diffmat = []
    for row_at in range(POLY):
        row_list = []
        for col_at in range(POLY):
            if row_at != col_at:
                row_list.append(values[row_at] / (values[col_at] * (gll_nodes[row_at] - gll_nodes[col_at])))
            elif row_at == 0:
                row_list.append(-degree * (degree + 1) / 4.0)
            elif row_at == degree:
                row_list.append(degree * (degree + 1) / 4.0)
            else:
                row_list.append(0.0)
        diffmat.append(row_list)
    return (jnp.asarray(gll_nodes, dtype=jnp.float32), jnp.asarray(weights, dtype=jnp.float32),
            jnp.asarray(diffmat, dtype=jnp.float32))


def derive(grid_field, diffmat, axis_at, flipped):
    matrix = diffmat.T if flipped else diffmat
    extent0, extent1, extent2 = grid_field.shape
    highest = lax.Precision.HIGHEST
    if axis_at == 0:
        blocks = grid_field.reshape(extent0 // POLY, POLY, extent1, extent2)
        result = jnp.einsum("ia,xayz->xiyz", matrix, blocks, precision=highest)
    elif axis_at == 1:
        blocks = grid_field.reshape(extent0, extent1 // POLY, POLY, extent2)
        result = jnp.einsum("ib,xybz->xyiz", matrix, blocks, precision=highest)
    else:
        blocks = grid_field.reshape(extent0, extent1, extent2 // POLY, POLY)
        result = jnp.einsum("xyzc,ic->xyzi", blocks, matrix, precision=highest)
    return result.reshape(grid_field.shape)


def along_axis(vector, axis_at):
    shape_at = [1, 1, 1]
    shape_at[axis_at] = vector.shape[0]
    return vector.reshape(shape_at)


def assemble(grid_field):
    running = grid_field
    nothing = jnp.zeros_like(grid_field)
    for axis_at in range(3):
        extent = running.shape[axis_at]
        node = lax.iota(jnp.int32, extent) % POLY
        first = along_axis(node == 0, axis_at)
        last = along_axis(node == POLY - 1, axis_at)
        widths = [(0, 0), (0, 0), (0, 0)]
        widths[axis_at] = (1, 1)
        padded = jnp.pad(running, widths)
        before = lax.slice_in_dim(padded, 0, extent, axis=axis_at)
        after = lax.slice_in_dim(padded, 2, extent + 2, axis=axis_at)
        running = running + jnp.where(first, before, nothing) + jnp.where(last, after, nothing)
    return running


def inverse_multiplicity(extent):
    node = lax.iota(jnp.int32, extent) % POLY
    position = lax.iota(jnp.int32, extent)
    inner_face = ((node == 0) & (position > 0)) | ((node == POLY - 1) & (position < extent - 1))
    return jnp.where(inner_face, 0.5, 1.0).astype(jnp.float32)


def apply_operator(grid_field, weight3, metric, diffmat):
    running = weight3 * grid_field
    for axis_at in range(3):
        running = running + derive(metric * derive(grid_field, diffmat, axis_at, False), diffmat, axis_at, True)
    return assemble(running)


def reference(velocity, coefficient, coords, forces, line_id, line_gain, dest_span, owner_element):
    abscissa, weights, diffmat = gll_tables()
    extent0, extent1, extent2 = coefficient.shape
    tile_zero = jnp.tile(weights, extent0 // POLY)
    tile_one = jnp.tile(weights, extent1 // POLY)
    tile_two = jnp.tile(weights, extent2 // POLY)
    weight3 = (tile_zero[:, None, None] * tile_one[None, :, None]) * tile_two[None, None, :]
    metric = weight3 * coefficient
    inv_mult = (inverse_multiplicity(extent0)[:, None, None] * inverse_multiplicity(extent1)[None, :, None]) * inverse_multiplicity(extent2)[None, None, :]

    gains = line_gain[line_id]
    scaled = forces * gains[None, :]
    kernels = []
    for dimension in range(3):
        kernels.append(jnp.exp(-(((abscissa[None, :] - coords[dimension][:, None]) / kernel_width) ** 2)))
    kernel3 = (kernels[0][:, :, None, None] * kernels[1][:, None, :, None]) * kernels[2][:, None, None, :]
    contrib = scaled.T[:, :, None, None, None] * kernel3[:, None]
    point_at = jnp.arange(coords.shape[1], dtype=jnp.int32)
    slab = point_at // SLAB_PTS
    target = dest_span[:, 0]
    elem_x = slab * EX + owner_element // (EY * EZ)
    elem_y = target * EY + (owner_element // EZ) % EY
    elem_z = owner_element % EZ
    elem_view = jnp.zeros((extent0 // POLY, extent1 // POLY, extent2 // POLY, 3, POLY, POLY, POLY), jnp.float32)
    elem_view = elem_view.at[elem_x, elem_y, elem_z].add(contrib)
    forcing = elem_view.transpose(3, 0, 4, 1, 5, 2, 6).reshape(3, extent0, extent1, extent2)

    running = derive(weight3 * (velocity[0] + forcing[0]), diffmat, 0, True)
    running = running + derive(weight3 * (velocity[1] + forcing[1]), diffmat, 1, True)
    running = running + derive(weight3 * (velocity[2] + forcing[2]), diffmat, 2, True)
    rhs = assemble(running)

    def weighted(first_vec, second_vec):
        return jnp.sum(first_vec * second_vec * inv_mult)

    pressure = jnp.zeros_like(rhs)
    residual = rhs
    direction = rhs
    norm_now = weighted(residual, residual)
    for iteration in range(ITERS):
        applied = apply_operator(direction, weight3, metric, diffmat)
        step_len = norm_now / weighted(direction, applied)
        pressure = pressure + step_len * direction
        residual = residual - step_len * applied
        norm_next = weighted(residual, residual)
        direction = residual + (norm_next / norm_now) * direction
        norm_now = norm_next
    return pressure, residual
```

```python
import jax
import jax.numpy as jnp
from jax import lax
from jax.sharding import PartitionSpec as P

POLY = 8
ITERS = 3


kernel_width = 0.45
gll_nodes = [
    -1.0,
    -0.8717401485096066,
    -0.5917001814331423,
    -0.2092992179024789,
    0.2092992179024789,
    0.5917001814331423,
    0.8717401485096066,
    1.0,
]


def with_halo(x, sides, width):
    for axis, dim in sides:
        size, length = (lax.axis_size(axis), x.shape[dim])
        up = [(i, (i + 1) % size) for i in range(size - 1)]
        down = [(j, i) for i, j in up]
        last = lax.slice_in_dim(x, length - width, length, axis=dim)
        first = lax.slice_in_dim(x, 0, width, axis=dim)
        before = lax.ppermute(last, axis, up)
        after = lax.ppermute(first, axis, down)
        x = jnp.concatenate([before, x, after], axis=dim)
    return x


def legendre_value(point, degree):
    previous = 1.0
    current = point
    for order in range(1, degree):
        following = ((2 * order + 1) * point * current - order * previous) / (order + 1)
        previous = current
        current = following
    return current


def gll_tables():
    degree = POLY - 1
    values = [legendre_value(point, degree) for point in gll_nodes]
    weights = [2.0 / (degree * (degree + 1) * value * value) for value in values]
    diffmat = []
    for row_at in range(POLY):
        row_list = []
        for col_at in range(POLY):
            if row_at != col_at:
                row_list.append(
                    values[row_at] / (values[col_at] * (gll_nodes[row_at] - gll_nodes[col_at]))
                )
            elif row_at == 0:
                row_list.append(-degree * (degree + 1) / 4.0)
            elif row_at == degree:
                row_list.append(degree * (degree + 1) / 4.0)
            else:
                row_list.append(0.0)
        diffmat.append(row_list)
    return (
        jnp.asarray(gll_nodes, dtype=jnp.float32),
        jnp.asarray(weights, dtype=jnp.float32),
        jnp.asarray(diffmat, dtype=jnp.float32),
    )


def derive(grid_field, diffmat, axis_at, flipped):
    matrix = diffmat.T if flipped else diffmat
    extent0, extent1, extent2 = grid_field.shape
    highest = lax.Precision.HIGHEST
    if axis_at == 0:
        blocks = grid_field.reshape(extent0 // POLY, POLY, extent1, extent2)
        result = jnp.einsum("ia,xayz->xiyz", matrix, blocks, precision=highest)
    elif axis_at == 1:
        blocks = grid_field.reshape(extent0, extent1 // POLY, POLY, extent2)
        result = jnp.einsum("ib,xybz->xyiz", matrix, blocks, precision=highest)
    else:
        block_width = 128
        tiled_matrix = jnp.kron(jnp.eye(block_width // POLY, dtype=jnp.float32), matrix)
        blocks = grid_field.reshape(extent0, extent1, extent2 // block_width, block_width)
        result = jnp.einsum("xyzc,ic->xyzi", blocks, tiled_matrix, precision=highest)
    return result.reshape(grid_field.shape)


def face_masks(extent):
    node = lax.iota(jnp.int32, extent) % POLY
    return (node == 0, node == POLY - 1)


def assemble(grid_field):
    extent0, extent1, extent2 = grid_field.shape
    first0, last0 = face_masks(extent0)
    first1, last1 = face_masks(extent1)
    first2, last2 = face_masks(extent2)
    first0, last0 = (first0[:, None, None], last0[:, None, None])
    first1, last1 = (first1[None, :, None], last1[None, :, None])
    first2, last2 = (first2[None, None, :], last2[None, None, :])
    nothing = jnp.zeros_like(grid_field)
    padded = with_halo(grid_field, (("stream", 0),), 1)
    running = (
        grid_field + jnp.where(first0, padded[:-2], nothing) + jnp.where(last0, padded[2:], nothing)
    )
    padded = with_halo(running, (("span", 1),), 1)
    running = (
        running
        + jnp.where(first1, padded[:, :-2], nothing)
        + jnp.where(last1, padded[:, 2:], nothing)
    )
    before = jnp.pad(running, ((0, 0), (0, 0), (1, 0)))[:, :, :-1]
    after = jnp.pad(running, ((0, 0), (0, 0), (0, 1)))[:, :, 1:]
    return running + jnp.where(first2, before, nothing) + jnp.where(last2, after, nothing)


def inverse_multiplicity(extent, offset, whole):
    node = lax.iota(jnp.int32, extent) % POLY
    position = offset + lax.iota(jnp.int32, extent)
    inner_face = (node == 0) & (position > 0) | (node == POLY - 1) & (position < whole - 1)
    return jnp.where(inner_face, 0.5, 1.0).astype(jnp.float32)


def butterfly_sum(values):
    for axis in ("span", "stream"):
        size = lax.axis_size(axis)
        if size & (size - 1):
            values = lax.psum(values, axis)
            continue
        stride = 1
        while stride < size:
            pairs = [(i, i ^ stride) for i in range(size)]
            values = values + lax.ppermute(values, axis, pairs)
            stride *= 2
    return values


def spread_points(arrived, abscissa, extent0, extent1, extent2):
    elems_y, elems_z = (extent1 // POLY, extent2 // POLY)
    kernels = []
    for dimension in range(3):
        kernels.append(
            jnp.exp(
                -(((abscissa[None, :] - arrived[:, dimension : dimension + 1]) / kernel_width) ** 2)
            )
        )
    element = arrived[:, 6].astype(jnp.int32) - 1
    valid = element >= 0
    elem_x = element // (elems_y * elems_z)
    elem_y = (element // elems_z) % elems_y
    elem_z = element % elems_z
    grid0 = lax.iota(jnp.int32, extent0)
    grid1 = lax.iota(jnp.int32, extent1)
    grid2 = lax.iota(jnp.int32, extent2)
    node0 = jnp.tile(kernels[0], (1, extent0 // POLY))
    node1 = jnp.tile(kernels[1], (1, extent1 // POLY))
    node2 = jnp.tile(kernels[2], (1, extent2 // POLY))
    along0 = jnp.where(elem_x[:, None] == grid0[None, :] // POLY, node0, 0.0)
    along1 = jnp.where(elem_y[:, None] == grid1[None, :] // POLY, node1, 0.0)
    along2 = jnp.where(
        valid[:, None] & (elem_z[:, None] == grid2[None, :] // POLY), node2, 0.0
    )
    left = arrived[:, 3:6][:, :, None, None] * (along0[:, None, :, None] * along1[:, None, None, :])
    return jnp.einsum("pcxy,pz->cxyz", left, along2, precision=lax.Precision.HIGHEST)


def project_points(coords, forces, line_id, line_gain, dest_span, owner_element, abscissa, extents):
    points_dev = coords.shape[1]
    spans = lax.axis_size("span")
    capacity = max(2, 2 * points_dev // spans)
    table_ids = lax.iota(jnp.int32, line_gain.shape[0])
    gains = jnp.sum(
        jnp.where(line_id[:, None] == table_ids[None, :], line_gain[None, :], 0.0), axis=1
    )
    scaled = forces * gains[None, :]
    target = dest_span[:, 0]
    owner_code = (owner_element + 1).astype(jnp.float32)
    payload = jnp.concatenate(
        [coords, scaled, owner_code[None, :], target.astype(jnp.float32)[None, :]], axis=0
    ).T
    order = lax.iota(jnp.int32, points_dev)
    earlier = (target[:, None] == target[None, :]) & (order[None, :] < order[:, None])
    ranks = jnp.sum(earlier.astype(jnp.int32), axis=1)
    slot_at = target * capacity + ranks
    outgoing = jnp.zeros((spans * capacity, 8), jnp.float32).at[slot_at].set(payload)
    outgoing = outgoing.reshape(spans, capacity, 8)
    arrived = lax.all_to_all(outgoing, "span", split_axis=0, concat_axis=0, tiled=True).reshape(
        spans * capacity, 8
    )
    return spread_points(arrived, abscissa, extents[0], extents[1], extents[2])


def local_operator(grid_field, weight3, metric, diffmat):
    running = weight3 * grid_field
    for axis_at in range(3):
        running = running + derive(
            metric * derive(grid_field, diffmat, axis_at, False), diffmat, axis_at, True
        )
    return running


def on_device(velocity, coefficient, coords, forces, line_id, line_gain, dest_span, owner_element):
    abscissa, weights, diffmat = gll_tables()
    extent0, extent1, extent2 = coefficient.shape
    tile_zero = jnp.tile(weights, extent0 // POLY)
    tile_one = jnp.tile(weights, extent1 // POLY)
    tile_two = jnp.tile(weights, extent2 // POLY)
    weight3 = tile_zero[:, None, None] * tile_one[None, :, None] * tile_two[None, None, :]
    metric = weight3 * coefficient
    inv_zero = inverse_multiplicity(
        extent0, lax.axis_index("stream") * extent0, extent0 * lax.axis_size("stream")
    )
    inv_one = inverse_multiplicity(
        extent1, lax.axis_index("span") * extent1, extent1 * lax.axis_size("span")
    )
    inv_two = inverse_multiplicity(extent2, 0, extent2)
    inv_mult = inv_zero[:, None, None] * inv_one[None, :, None] * inv_two[None, None, :]
    forcing = project_points(
        coords,
        forces,
        line_id,
        line_gain,
        dest_span,
        owner_element,
        abscissa,
        (extent0, extent1, extent2),
    )
    running = derive(weight3 * (velocity[0] + forcing[0]), diffmat, 0, True)
    running = running + derive(weight3 * (velocity[1] + forcing[1]), diffmat, 1, True)
    running = running + derive(weight3 * (velocity[2] + forcing[2]), diffmat, 2, True)
    rhs = assemble(running)

    def weighted(first_vec, second_vec):
        return jnp.sum(first_vec * second_vec * inv_mult)

    pressure = jnp.zeros_like(rhs)
    residual = rhs
    direction = rhs
    local = local_operator(residual, weight3, metric, diffmat)
    sums = butterfly_sum(jnp.stack([weighted(residual, residual), jnp.sum(residual * local)]))
    norm_now, curvature = sums[0], sums[1]
    searched = assemble(local)
    step_len = norm_now / curvature
    for iteration in range(1, ITERS + 1):
        pressure = pressure + step_len * direction
        residual = residual - step_len * searched
        if iteration == ITERS:
            break
        local = local_operator(residual, weight3, metric, diffmat)
        sums = butterfly_sum(
            jnp.stack(
                [
                    weighted(residual, residual),
                    jnp.sum(residual * local),
                    weighted(residual, searched),
                ]
            )
        )
        applied = assemble(local)
        norm_next, own_curvature, cross = sums[0], sums[1], sums[2]
        ratio = norm_next / norm_now
        direction = residual + ratio * direction
        searched = applied + ratio * searched
        curvature = own_curvature + 2.0 * ratio * cross + ratio * ratio * curvature
        norm_now = norm_next
        step_len = norm_now / curvature
    return (pressure, residual)


def solution(mesh):
    return jax.shard_map(
        on_device,
        mesh=mesh,
        in_specs=(
            P(None, "stream", "span", None),
            P("stream", "span", None),
            P(None, ("stream", "span")),
            P(None, ("stream", "span")),
            P(("stream", "span")),
            P(),
            P(("stream", "span"), None),
            P(("stream", "span")),
        ),
        out_specs=(P("stream", "span", None), P("stream", "span", None)),
        check_vma=False,
    )
```

```python
import jax
import jax.numpy as jnp
from jax import lax
from jax.sharding import PartitionSpec as P

POLY = 8
ITERS = 3


kernel_width = 0.45
gll_nodes = [
    -1.0,
    -0.8717401485096066,
    -0.5917001814331423,
    -0.2092992179024789,
    0.2092992179024789,
    0.5917001814331423,
    0.8717401485096066,
    1.0,
]


def with_halo(x, sides, width):
    for axis, dim in sides:
        size, length = (lax.axis_size(axis), x.shape[dim])
        up = [(i, (i + 1) % size) for i in range(size - 1)]
        down = [(j, i) for i, j in up]
        last = lax.slice_in_dim(x, length - width, length, axis=dim)
        first = lax.slice_in_dim(x, 0, width, axis=dim)
        before = lax.ppermute(last, axis, up)
        after = lax.ppermute(first, axis, down)
        x = jnp.concatenate([before, x, after], axis=dim)
    return x


def legendre_value(point, degree):
    previous = 1.0
    current = point
    for order in range(1, degree):
        following = ((2 * order + 1) * point * current - order * previous) / (order + 1)
        previous = current
        current = following
    return current


def gll_tables():
    degree = POLY - 1
    values = [legendre_value(point, degree) for point in gll_nodes]
    weights = [2.0 / (degree * (degree + 1) * value * value) for value in values]
    diffmat = []
    for row_at in range(POLY):
        row_list = []
        for col_at in range(POLY):
            if row_at != col_at:
                row_list.append(
                    values[row_at] / (values[col_at] * (gll_nodes[row_at] - gll_nodes[col_at]))
                )
            elif row_at == 0:
                row_list.append(-degree * (degree + 1) / 4.0)
            elif row_at == degree:
                row_list.append(degree * (degree + 1) / 4.0)
            else:
                row_list.append(0.0)
        diffmat.append(row_list)
    return (
        jnp.asarray(gll_nodes, dtype=jnp.float32),
        jnp.asarray(weights, dtype=jnp.float32),
        jnp.asarray(diffmat, dtype=jnp.float32),
    )


def derive(grid_field, diffmat, axis_at, flipped):
    matrix = diffmat.T if flipped else diffmat
    extent0, extent1, extent2 = grid_field.shape
    highest = lax.Precision.HIGHEST
    if axis_at == 0:
        blocks = grid_field.reshape(extent0 // POLY, POLY, extent1, extent2)
        result = jnp.einsum("ia,xayz->xiyz", matrix, blocks, precision=highest)
    elif axis_at == 1:
        blocks = grid_field.reshape(extent0, extent1 // POLY, POLY, extent2)
        result = jnp.einsum("ib,xybz->xyiz", matrix, blocks, precision=highest)
    else:
        block_width = 128
        tiled_matrix = jnp.kron(jnp.eye(block_width // POLY, dtype=jnp.float32), matrix)
        blocks = grid_field.reshape(extent0, extent1, extent2 // block_width, block_width)
        result = jnp.einsum("xyzc,ic->xyzi", blocks, tiled_matrix, precision=highest)
    return result.reshape(grid_field.shape)


def face_masks(extent):
    node = lax.iota(jnp.int32, extent) % POLY
    return (node == 0, node == POLY - 1)


def assemble(grid_field):
    extent0, extent1, extent2 = grid_field.shape
    first0, last0 = face_masks(extent0)
    first1, last1 = face_masks(extent1)
    first2, last2 = face_masks(extent2)
    first0, last0 = (first0[:, None, None], last0[:, None, None])
    first1, last1 = (first1[None, :, None], last1[None, :, None])
    first2, last2 = (first2[None, None, :], last2[None, None, :])
    nothing = jnp.zeros_like(grid_field)
    padded = with_halo(grid_field, (("stream", 0),), 1)
    running = (
        grid_field + jnp.where(first0, padded[:-2], nothing) + jnp.where(last0, padded[2:], nothing)
    )
    padded = with_halo(running, (("span", 1),), 1)
    running = (
        running
        + jnp.where(first1, padded[:, :-2], nothing)
        + jnp.where(last1, padded[:, 2:], nothing)
    )
    before = jnp.pad(running, ((0, 0), (0, 0), (1, 0)))[:, :, :-1]
    after = jnp.pad(running, ((0, 0), (0, 0), (0, 1)))[:, :, 1:]
    return running + jnp.where(first2, before, nothing) + jnp.where(last2, after, nothing)


def inverse_multiplicity(extent, offset, whole):
    node = lax.iota(jnp.int32, extent) % POLY
    position = offset + lax.iota(jnp.int32, extent)
    inner_face = (node == 0) & (position > 0) | (node == POLY - 1) & (position < whole - 1)
    return jnp.where(inner_face, 0.5, 1.0).astype(jnp.float32)


def mesh_sum(values):
    axes = ("stream", "span")
    count = lax.axis_size(axes)
    spread = jnp.broadcast_to(values[None], (count,) + values.shape)
    gathered = lax.all_to_all(spread, axes, 0, 0, tiled=True)
    return jnp.sum(gathered, axis=0)


def spread_points(arrived, abscissa, extent0, extent1, extent2):
    elems_y, elems_z = (extent1 // POLY, extent2 // POLY)
    kernels = []
    for dimension in range(3):
        kernels.append(
            jnp.exp(
                -(((abscissa[None, :] - arrived[:, dimension : dimension + 1]) / kernel_width) ** 2)
            )
        )
    element = arrived[:, 6].astype(jnp.int32) - 1
    valid = element >= 0
    elem_x = element // (elems_y * elems_z)
    elem_y = (element // elems_z) % elems_y
    elem_z = element % elems_z
    grid0 = lax.iota(jnp.int32, extent0)
    grid1 = lax.iota(jnp.int32, extent1)
    grid2 = lax.iota(jnp.int32, extent2)
    node0 = jnp.tile(kernels[0], (1, extent0 // POLY))
    node1 = jnp.tile(kernels[1], (1, extent1 // POLY))
    node2 = jnp.tile(kernels[2], (1, extent2 // POLY))
    along0 = jnp.where(elem_x[:, None] == grid0[None, :] // POLY, node0, 0.0)
    along1 = jnp.where(elem_y[:, None] == grid1[None, :] // POLY, node1, 0.0)
    along2 = jnp.where(
        valid[:, None] & (elem_z[:, None] == grid2[None, :] // POLY), node2, 0.0
    )
    left = arrived[:, 3:6][:, :, None, None] * (along0[:, None, :, None] * along1[:, None, None, :])
    return jnp.einsum("pcxy,pz->cxyz", left, along2, precision=lax.Precision.HIGHEST)


def project_points(coords, forces, line_id, line_gain, dest_span, owner_element, abscissa, extents):
    points_dev = coords.shape[1]
    spans = lax.axis_size("span")
    capacity = max(2, 2 * points_dev // spans)
    table_ids = lax.iota(jnp.int32, line_gain.shape[0])
    gains = jnp.sum(
        jnp.where(line_id[:, None] == table_ids[None, :], line_gain[None, :], 0.0), axis=1
    )
    scaled = forces * gains[None, :]
    target = dest_span[:, 0]
    owner_code = (owner_element + 1).astype(jnp.float32)
    payload = jnp.concatenate(
        [coords, scaled, owner_code[None, :], target.astype(jnp.float32)[None, :]], axis=0
    ).T
    order = lax.iota(jnp.int32, points_dev)
    earlier = (target[:, None] == target[None, :]) & (order[None, :] < order[:, None])
    ranks = jnp.sum(earlier.astype(jnp.int32), axis=1)
    slot_at = target * capacity + ranks
    outgoing = jnp.zeros((spans * capacity, 8), jnp.float32).at[slot_at].set(payload)
    outgoing = outgoing.reshape(spans, capacity, 8)
    arrived = lax.all_to_all(outgoing, "span", split_axis=0, concat_axis=0, tiled=True).reshape(
        spans * capacity, 8
    )
    return spread_points(arrived, abscissa, extents[0], extents[1], extents[2])


def local_operator(grid_field, weight3, metric, diffmat):
    running = weight3 * grid_field
    for axis_at in range(3):
        running = running + derive(
            metric * derive(grid_field, diffmat, axis_at, False), diffmat, axis_at, True
        )
    return running


def on_device(velocity, coefficient, coords, forces, line_id, line_gain, dest_span, owner_element):
    abscissa, weights, diffmat = gll_tables()
    extent0, extent1, extent2 = coefficient.shape
    tile_zero = jnp.tile(weights, extent0 // POLY)
    tile_one = jnp.tile(weights, extent1 // POLY)
    tile_two = jnp.tile(weights, extent2 // POLY)
    weight3 = tile_zero[:, None, None] * tile_one[None, :, None] * tile_two[None, None, :]
    metric = weight3 * coefficient
    inv_zero = inverse_multiplicity(
        extent0, lax.axis_index("stream") * extent0, extent0 * lax.axis_size("stream")
    )
    inv_one = inverse_multiplicity(
        extent1, lax.axis_index("span") * extent1, extent1 * lax.axis_size("span")
    )
    inv_two = inverse_multiplicity(extent2, 0, extent2)
    inv_mult = inv_zero[:, None, None] * inv_one[None, :, None] * inv_two[None, None, :]
    forcing = project_points(
        coords,
        forces,
        line_id,
        line_gain,
        dest_span,
        owner_element,
        abscissa,
        (extent0, extent1, extent2),
    )
    running = derive(weight3 * (velocity[0] + forcing[0]), diffmat, 0, True)
    running = running + derive(weight3 * (velocity[1] + forcing[1]), diffmat, 1, True)
    running = running + derive(weight3 * (velocity[2] + forcing[2]), diffmat, 2, True)
    rhs = assemble(running)

    def weighted(first_vec, second_vec):
        return jnp.sum(first_vec * second_vec * inv_mult)

    pressure = jnp.zeros_like(rhs)
    residual = rhs
    direction = rhs
    local = local_operator(residual, weight3, metric, diffmat)
    sums = mesh_sum(jnp.stack([weighted(residual, residual), jnp.sum(residual * local)]))
    norm_now, curvature = sums[0], sums[1]
    searched = assemble(local)
    step_len = norm_now / curvature
    for iteration in range(1, ITERS + 1):
        pressure = pressure + step_len * direction
        residual = residual - step_len * searched
        if iteration == ITERS:
            break
        local = local_operator(residual, weight3, metric, diffmat)
        sums = mesh_sum(
            jnp.stack(
                [
                    weighted(residual, residual),
                    jnp.sum(residual * local),
                    weighted(residual, searched),
                ]
            )
        )
        applied = assemble(local)
        norm_next, own_curvature, cross = sums[0], sums[1], sums[2]
        ratio = norm_next / norm_now
        direction = residual + ratio * direction
        searched = applied + ratio * searched
        curvature = own_curvature + 2.0 * ratio * cross + ratio * ratio * curvature
        norm_now = norm_next
        step_len = norm_now / curvature
    return (pressure, residual)


def solution(mesh):
    return jax.shard_map(
        on_device,
        mesh=mesh,
        in_specs=(
            P(None, "stream", "span", None),
            P("stream", "span", None),
            P(None, ("stream", "span")),
            P(None, ("stream", "span")),
            P(("stream", "span")),
            P(),
            P(("stream", "span"), None),
            P(("stream", "span")),
        ),
        out_specs=(P("stream", "span", None), P("stream", "span", None)),
        check_vma=False,
    )
```

```python
import jax
import jax.numpy as jnp
from jax import lax
from jax.sharding import PartitionSpec as P

POLY = 8
ITERS = 3


kernel_width = 0.45
gll_nodes = [
    -1.0,
    -0.8717401485096066,
    -0.5917001814331423,
    -0.2092992179024789,
    0.2092992179024789,
    0.5917001814331423,
    0.8717401485096066,
    1.0,
]


def legendre_value(point, degree):
    previous = 1.0
    current = point
    for order in range(1, degree):
        following = ((2 * order + 1) * point * current - order * previous) / (order + 1)
        previous = current
        current = following
    return current


def gll_tables():
    degree = POLY - 1
    values = [legendre_value(point, degree) for point in gll_nodes]
    weights = [2.0 / (degree * (degree + 1) * value * value) for value in values]
    diffmat = []
    for row_at in range(POLY):
        row_list = []
        for col_at in range(POLY):
            if row_at != col_at:
                row_list.append(
                    values[row_at] / (values[col_at] * (gll_nodes[row_at] - gll_nodes[col_at]))
                )
            elif row_at == 0:
                row_list.append(-degree * (degree + 1) / 4.0)
            elif row_at == degree:
                row_list.append(degree * (degree + 1) / 4.0)
            else:
                row_list.append(0.0)
        diffmat.append(row_list)
    return (
        jnp.asarray(gll_nodes, dtype=jnp.float32),
        jnp.asarray(weights, dtype=jnp.float32),
        jnp.asarray(diffmat, dtype=jnp.float32),
    )


def derive(grid_field, diffmat, axis_at, flipped):
    matrix = diffmat.T if flipped else diffmat
    extent0, extent1, extent2 = grid_field.shape
    highest = lax.Precision.HIGHEST
    if axis_at == 0:
        blocks = grid_field.reshape(extent0 // POLY, POLY, extent1, extent2)
        result = jnp.einsum("ia,xayz->xiyz", matrix, blocks, precision=highest)
    elif axis_at == 1:
        blocks = grid_field.reshape(extent0, extent1 // POLY, POLY, extent2)
        result = jnp.einsum("ib,xybz->xyiz", matrix, blocks, precision=highest)
    else:
        block_width = 128
        tiled_matrix = jnp.kron(jnp.eye(block_width // POLY, dtype=jnp.float32), matrix)
        blocks = grid_field.reshape(extent0, extent1, extent2 // block_width, block_width)
        result = jnp.einsum("xyzc,ic->xyzi", blocks, tiled_matrix, precision=highest)
    return result.reshape(grid_field.shape)


def face_masks(extent):
    node = lax.iota(jnp.int32, extent) % POLY
    return (node == 0, node == POLY - 1)


def shifted(block, step0, step1):
    size0, size1 = (lax.axis_size("stream"), lax.axis_size("span"))
    pairs = [
        (i * size1 + j, (i + step0) * size1 + (j + step1))
        for i in range(size0)
        for j in range(size1)
        if 0 <= i + step0 < size0 and 0 <= j + step1 < size1
    ]
    return lax.ppermute(block, ("stream", "span"), pairs)


def add_faces(field, before, after, first, last, dim):
    nothing = jnp.zeros_like(field)
    length = field.shape[dim]
    below = jnp.concatenate([before, lax.slice_in_dim(field, 0, length - 1, axis=dim)], axis=dim)
    above = jnp.concatenate([lax.slice_in_dim(field, 1, length, axis=dim), after], axis=dim)
    return field + jnp.where(first, below, nothing) + jnp.where(last, above, nothing)


def assemble_once(grid_field):
    extent0, extent1, extent2 = grid_field.shape
    first0, last0 = face_masks(extent0)
    first1, last1 = face_masks(extent1)
    first2, last2 = face_masks(extent2)
    first0, last0 = (first0[:, None, None], last0[:, None, None])
    first1, last1 = (first1[None, :, None], last1[None, :, None])
    first2, last2 = (first2[None, None, :], last2[None, None, :])
    low0, high0 = (grid_field[:1], grid_field[-1:])
    low1, high1 = (grid_field[:, :1], grid_field[:, -1:])
    prev0 = shifted(high0, 1, 0)
    next0 = shifted(low0, -1, 0)
    prev1 = shifted(high1, 0, 1)
    next1 = shifted(low1, 0, -1)
    prev1_prev0 = shifted(high1[-1:], 1, 1)
    prev1_next0 = shifted(high1[:1], -1, 1)
    next1_prev0 = shifted(low1[-1:], 1, -1)
    next1_next0 = shifted(low1[:1], -1, -1)
    running = add_faces(grid_field, prev0, next0, first0, last0, 0)
    prev1 = add_faces(prev1, prev1_prev0, prev1_next0, first0, last0, 0)
    next1 = add_faces(next1, next1_prev0, next1_next0, first0, last0, 0)
    running = add_faces(running, prev1, next1, first1, last1, 1)
    nothing = jnp.zeros_like(grid_field)
    before = jnp.pad(running, ((0, 0), (0, 0), (1, 0)))[:, :, :-1]
    after = jnp.pad(running, ((0, 0), (0, 0), (0, 1)))[:, :, 1:]
    return running + jnp.where(first2, before, nothing) + jnp.where(last2, after, nothing)


def assemble(grid_field):
    extent0, extent1, extent2 = grid_field.shape
    first0, last0 = face_masks(extent0)
    first1, last1 = face_masks(extent1)
    first2, last2 = face_masks(extent2)
    first0, last0 = (first0[:, None, None], last0[:, None, None])
    first1, last1 = (first1[None, :, None], last1[None, :, None])
    first2, last2 = (first2[None, None, :], last2[None, None, :])
    prev1 = shifted(grid_field[:, -1:], 0, 1)
    next1 = shifted(grid_field[:, :1], 0, -1)
    running = add_faces(grid_field, prev1, next1, first1, last1, 1)
    prev0 = shifted(running[-1:], 1, 0)
    next0 = shifted(running[:1], -1, 0)
    running = add_faces(running, prev0, next0, first0, last0, 0)
    nothing = jnp.zeros_like(grid_field)
    before = jnp.pad(running, ((0, 0), (0, 0), (1, 0)))[:, :, :-1]
    after = jnp.pad(running, ((0, 0), (0, 0), (0, 1)))[:, :, 1:]
    return running + jnp.where(first2, before, nothing) + jnp.where(last2, after, nothing)


def inverse_multiplicity(extent, offset, whole):
    node = lax.iota(jnp.int32, extent) % POLY
    position = offset + lax.iota(jnp.int32, extent)
    inner_face = (node == 0) & (position > 0) | (node == POLY - 1) & (position < whole - 1)
    return jnp.where(inner_face, 0.5, 1.0).astype(jnp.float32)


def mesh_sum(values):
    axes = ("stream", "span")
    count = lax.axis_size(axes)
    spread = jnp.broadcast_to(values[None], (count,) + values.shape)
    gathered = lax.all_to_all(spread, axes, 0, 0, tiled=True)
    return jnp.sum(gathered, axis=0)


def spread_points(arrived, abscissa, extent0, extent1, extent2):
    elems_y, elems_z = (extent1 // POLY, extent2 // POLY)
    kernels = []
    for dimension in range(3):
        kernels.append(
            jnp.exp(
                -(((abscissa[None, :] - arrived[:, dimension : dimension + 1]) / kernel_width) ** 2)
            )
        )
    element = arrived[:, 6].astype(jnp.int32) - 1
    valid = element >= 0
    elem_x = element // (elems_y * elems_z)
    elem_y = (element // elems_z) % elems_y
    elem_z = element % elems_z
    grid0 = lax.iota(jnp.int32, extent0)
    grid1 = lax.iota(jnp.int32, extent1)
    grid2 = lax.iota(jnp.int32, extent2)
    node0 = jnp.tile(kernels[0], (1, extent0 // POLY))
    node1 = jnp.tile(kernels[1], (1, extent1 // POLY))
    node2 = jnp.tile(kernels[2], (1, extent2 // POLY))
    along0 = jnp.where(elem_x[:, None] == grid0[None, :] // POLY, node0, 0.0)
    along1 = jnp.where(elem_y[:, None] == grid1[None, :] // POLY, node1, 0.0)
    along2 = jnp.where(
        valid[:, None] & (elem_z[:, None] == grid2[None, :] // POLY), node2, 0.0
    )
    left = arrived[:, 3:6][:, :, None, None] * (along0[:, None, :, None] * along1[:, None, None, :])
    return jnp.einsum("pcxy,pz->cxyz", left, along2, precision=lax.Precision.HIGHEST)


def project_points(coords, forces, line_id, line_gain, dest_span, owner_element, abscissa, extents):
    points_dev = coords.shape[1]
    spans = lax.axis_size("span")
    capacity = max(2, 2 * points_dev // spans)
    table_ids = lax.iota(jnp.int32, line_gain.shape[0])
    gains = jnp.sum(
        jnp.where(line_id[:, None] == table_ids[None, :], line_gain[None, :], 0.0), axis=1
    )
    scaled = forces * gains[None, :]
    target = dest_span[:, 0]
    owner_code = (owner_element + 1).astype(jnp.float32)
    payload = jnp.concatenate(
        [coords, scaled, owner_code[None, :], target.astype(jnp.float32)[None, :]], axis=0
    ).T
    order = lax.iota(jnp.int32, points_dev)
    earlier = (target[:, None] == target[None, :]) & (order[None, :] < order[:, None])
    ranks = jnp.sum(earlier.astype(jnp.int32), axis=1)
    slot_at = target * capacity + ranks
    outgoing = jnp.zeros((spans * capacity, 8), jnp.float32).at[slot_at].set(payload)
    outgoing = outgoing.reshape(spans, capacity, 8)
    arrived = lax.all_to_all(outgoing, "span", split_axis=0, concat_axis=0, tiled=True).reshape(
        spans * capacity, 8
    )
    return spread_points(arrived, abscissa, extents[0], extents[1], extents[2])


def local_operator(grid_field, weight3, metric, diffmat):
    running = weight3 * grid_field
    for axis_at in range(3):
        running = running + derive(
            metric * derive(grid_field, diffmat, axis_at, False), diffmat, axis_at, True
        )
    return running


def on_device(velocity, coefficient, coords, forces, line_id, line_gain, dest_span, owner_element):
    abscissa, weights, diffmat = gll_tables()
    extent0, extent1, extent2 = coefficient.shape
    tile_zero = jnp.tile(weights, extent0 // POLY)
    tile_one = jnp.tile(weights, extent1 // POLY)
    tile_two = jnp.tile(weights, extent2 // POLY)
    weight3 = tile_zero[:, None, None] * tile_one[None, :, None] * tile_two[None, None, :]
    metric = weight3 * coefficient
    inv_zero = inverse_multiplicity(
        extent0, lax.axis_index("stream") * extent0, extent0 * lax.axis_size("stream")
    )
    inv_one = inverse_multiplicity(
        extent1, lax.axis_index("span") * extent1, extent1 * lax.axis_size("span")
    )
    inv_two = inverse_multiplicity(extent2, 0, extent2)
    inv_mult = inv_zero[:, None, None] * inv_one[None, :, None] * inv_two[None, None, :]
    forcing = project_points(
        coords,
        forces,
        line_id,
        line_gain,
        dest_span,
        owner_element,
        abscissa,
        (extent0, extent1, extent2),
    )
    running = derive(weight3 * (velocity[0] + forcing[0]), diffmat, 0, True)
    running = running + derive(weight3 * (velocity[1] + forcing[1]), diffmat, 1, True)
    running = running + derive(weight3 * (velocity[2] + forcing[2]), diffmat, 2, True)
    rhs = assemble_once(running)

    def weighted(first_vec, second_vec):
        return jnp.sum(first_vec * second_vec * inv_mult)

    pressure = jnp.zeros_like(rhs)
    residual = rhs
    direction = rhs
    local = local_operator(residual, weight3, metric, diffmat)
    sums = mesh_sum(jnp.stack([weighted(residual, residual), jnp.sum(residual * local)]))
    norm_now, curvature = sums[0], sums[1]
    searched = assemble(local)
    step_len = norm_now / curvature
    for iteration in range(1, ITERS + 1):
        pressure = pressure + step_len * direction
        residual = residual - step_len * searched
        if iteration == ITERS:
            break
        local = local_operator(residual, weight3, metric, diffmat)
        sums = mesh_sum(
            jnp.stack(
                [
                    weighted(residual, residual),
                    jnp.sum(residual * local),
                    weighted(residual, searched),
                ]
            )
        )
        applied = assemble(local)
        norm_next, own_curvature, cross = sums[0], sums[1], sums[2]
        ratio = norm_next / norm_now
        direction = residual + ratio * direction
        searched = applied + ratio * searched
        curvature = own_curvature + 2.0 * ratio * cross + ratio * ratio * curvature
        norm_now = norm_next
        step_len = norm_now / curvature
    return (pressure, residual)


def solution(mesh):
    return jax.shard_map(
        on_device,
        mesh=mesh,
        in_specs=(
            P(None, "stream", "span", None),
            P("stream", "span", None),
            P(None, ("stream", "span")),
            P(None, ("stream", "span")),
            P(("stream", "span")),
            P(),
            P(("stream", "span"), None),
            P(("stream", "span")),
        ),
        out_specs=(P("stream", "span", None), P("stream", "span", None)),
        check_vma=False,
    )
```

```python
import jax
import jax.numpy as jnp
from jax import lax
from jax.sharding import PartitionSpec as P

POLY = 8
ITERS = 3


kernel_width = 0.45
gll_nodes = [
    -1.0,
    -0.8717401485096066,
    -0.5917001814331423,
    -0.2092992179024789,
    0.2092992179024789,
    0.5917001814331423,
    0.8717401485096066,
    1.0,
]


def with_halo(x, sides, width):
    for axis, dim in sides:
        size, length = (lax.axis_size(axis), x.shape[dim])
        up = [(i, (i + 1) % size) for i in range(size - 1)]
        down = [(j, i) for i, j in up]
        last = lax.slice_in_dim(x, length - width, length, axis=dim)
        first = lax.slice_in_dim(x, 0, width, axis=dim)
        before = lax.ppermute(last, axis, up)
        after = lax.ppermute(first, axis, down)
        x = jnp.concatenate([before, x, after], axis=dim)
    return x


def legendre_value(point, degree):
    previous = 1.0
    current = point
    for order in range(1, degree):
        following = ((2 * order + 1) * point * current - order * previous) / (order + 1)
        previous = current
        current = following
    return current


def gll_tables():
    degree = POLY - 1
    values = [legendre_value(point, degree) for point in gll_nodes]
    weights = [2.0 / (degree * (degree + 1) * value * value) for value in values]
    diffmat = []
    for row_at in range(POLY):
        row_list = []
        for col_at in range(POLY):
            if row_at != col_at:
                row_list.append(
                    values[row_at] / (values[col_at] * (gll_nodes[row_at] - gll_nodes[col_at]))
                )
            elif row_at == 0:
                row_list.append(-degree * (degree + 1) / 4.0)
            elif row_at == degree:
                row_list.append(degree * (degree + 1) / 4.0)
            else:
                row_list.append(0.0)
        diffmat.append(row_list)
    return (
        jnp.asarray(gll_nodes, dtype=jnp.float32),
        jnp.asarray(weights, dtype=jnp.float32),
        jnp.asarray(diffmat, dtype=jnp.float32),
    )


def derive(grid_field, diffmat, axis_at, flipped):
    matrix = diffmat.T if flipped else diffmat
    extent0, extent1, extent2 = grid_field.shape
    highest = lax.Precision.HIGHEST
    if axis_at == 0:
        blocks = grid_field.reshape(extent0 // POLY, POLY, extent1, extent2)
        result = jnp.einsum("ia,xayz->xiyz", matrix, blocks, precision=highest)
    elif axis_at == 1:
        blocks = grid_field.reshape(extent0, extent1 // POLY, POLY, extent2)
        result = jnp.einsum("ib,xybz->xyiz", matrix, blocks, precision=highest)
    else:
        block_width = 128
        tiled_matrix = jnp.kron(jnp.eye(block_width // POLY, dtype=jnp.float32), matrix)
        blocks = grid_field.reshape(extent0, extent1, extent2 // block_width, block_width)
        result = jnp.einsum("xyzc,ic->xyzi", blocks, tiled_matrix, precision=highest)
    return result.reshape(grid_field.shape)


def face_masks(extent):
    node = lax.iota(jnp.int32, extent) % POLY
    return (node == 0, node == POLY - 1)


def assemble(grid_field):
    extent0, extent1, extent2 = grid_field.shape
    first0, last0 = face_masks(extent0)
    first1, last1 = face_masks(extent1)
    first2, last2 = face_masks(extent2)
    first0, last0 = (first0[:, None, None], last0[:, None, None])
    first1, last1 = (first1[None, :, None], last1[None, :, None])
    first2, last2 = (first2[None, None, :], last2[None, None, :])
    nothing = jnp.zeros_like(grid_field)
    padded = with_halo(grid_field, (("stream", 0),), 1)
    running = (
        grid_field + jnp.where(first0, padded[:-2], nothing) + jnp.where(last0, padded[2:], nothing)
    )
    padded = with_halo(running, (("span", 1),), 1)
    running = (
        running
        + jnp.where(first1, padded[:, :-2], nothing)
        + jnp.where(last1, padded[:, 2:], nothing)
    )
    before = jnp.pad(running, ((0, 0), (0, 0), (1, 0)))[:, :, :-1]
    after = jnp.pad(running, ((0, 0), (0, 0), (0, 1)))[:, :, 1:]
    return running + jnp.where(first2, before, nothing) + jnp.where(last2, after, nothing)


def inverse_multiplicity(extent, offset, whole):
    node = lax.iota(jnp.int32, extent) % POLY
    position = offset + lax.iota(jnp.int32, extent)
    inner_face = (node == 0) & (position > 0) | (node == POLY - 1) & (position < whole - 1)
    return jnp.where(inner_face, 0.5, 1.0).astype(jnp.float32)


def mesh_sum(values):
    axes = ("stream", "span")
    count = lax.axis_size(axes)
    spread = jnp.broadcast_to(values[None], (count,) + values.shape)
    gathered = lax.all_to_all(spread, axes, 0, 0, tiled=True)
    return jnp.sum(gathered, axis=0)


def spread_points(arrived, abscissa, extent0, extent1, extent2):
    elems_y, elems_z = (extent1 // POLY, extent2 // POLY)
    kernels = []
    for dimension in range(3):
        kernels.append(
            jnp.exp(
                -(((abscissa[None, :] - arrived[:, dimension : dimension + 1]) / kernel_width) ** 2)
            )
        )
    element = arrived[:, 6].astype(jnp.int32) - 1
    valid = element >= 0
    elem_x = element // (elems_y * elems_z)
    elem_y = (element // elems_z) % elems_y
    elem_z = element % elems_z
    grid0 = lax.iota(jnp.int32, extent0)
    grid1 = lax.iota(jnp.int32, extent1)
    grid2 = lax.iota(jnp.int32, extent2)
    node0 = jnp.tile(kernels[0], (1, extent0 // POLY))
    node1 = jnp.tile(kernels[1], (1, extent1 // POLY))
    node2 = jnp.tile(kernels[2], (1, extent2 // POLY))
    along0 = jnp.where(elem_x[:, None] == grid0[None, :] // POLY, node0, 0.0)
    along1 = jnp.where(elem_y[:, None] == grid1[None, :] // POLY, node1, 0.0)
    along2 = jnp.where(
        valid[:, None] & (elem_z[:, None] == grid2[None, :] // POLY), node2, 0.0
    )
    left = arrived[:, 3:6][:, :, None, None] * (along0[:, None, :, None] * along1[:, None, None, :])
    return jnp.einsum("pcxy,pz->cxyz", left, along2, precision=lax.Precision.HIGHEST)


def project_points(coords, forces, line_id, line_gain, dest_span, owner_element, abscissa, extents):
    points_dev = coords.shape[1]
    spans = lax.axis_size("span")
    capacity = max(2, 2 * points_dev // spans)
    table_ids = lax.iota(jnp.int32, line_gain.shape[0])
    gains = jnp.sum(
        jnp.where(line_id[:, None] == table_ids[None, :], line_gain[None, :], 0.0), axis=1
    )
    scaled = forces * gains[None, :]
    target = dest_span[:, 0]
    owner_code = (owner_element + 1).astype(jnp.float32)
    payload = jnp.concatenate(
        [coords, scaled, owner_code[None, :], target.astype(jnp.float32)[None, :]], axis=0
    ).T
    order = lax.iota(jnp.int32, points_dev)
    earlier = (target[:, None] == target[None, :]) & (order[None, :] < order[:, None])
    ranks = jnp.sum(earlier.astype(jnp.int32), axis=1)
    slot_at = target * capacity + ranks
    outgoing = jnp.zeros((spans * capacity, 8), jnp.float32).at[slot_at].set(payload)
    outgoing = outgoing.reshape(spans, capacity, 8)
    arrived = lax.all_to_all(outgoing, "span", split_axis=0, concat_axis=0, tiled=True).reshape(
        spans * capacity, 8
    )
    return spread_points(arrived, abscissa, extents[0], extents[1], extents[2])


def local_operator(grid_field, weight3, metric, diffmat):
    running = weight3 * grid_field
    for axis_at in range(3):
        running = running + derive(
            metric * derive(grid_field, diffmat, axis_at, False), diffmat, axis_at, True
        )
    return running


def on_device(velocity, coefficient, coords, forces, line_id, line_gain, dest_span, owner_element):
    abscissa, weights, diffmat = gll_tables()
    extent0, extent1, extent2 = coefficient.shape
    tile_zero = jnp.tile(weights, extent0 // POLY)
    tile_one = jnp.tile(weights, extent1 // POLY)
    tile_two = jnp.tile(weights, extent2 // POLY)
    weight3 = tile_zero[:, None, None] * tile_one[None, :, None] * tile_two[None, None, :]
    metric = weight3 * coefficient
    inv_zero = inverse_multiplicity(
        extent0, lax.axis_index("stream") * extent0, extent0 * lax.axis_size("stream")
    )
    inv_one = inverse_multiplicity(
        extent1, lax.axis_index("span") * extent1, extent1 * lax.axis_size("span")
    )
    inv_two = inverse_multiplicity(extent2, 0, extent2)
    inv_mult = inv_zero[:, None, None] * inv_one[None, :, None] * inv_two[None, None, :]
    forcing = project_points(
        coords,
        forces,
        line_id,
        line_gain,
        dest_span,
        owner_element,
        abscissa,
        (extent0, extent1, extent2),
    )
    running = derive(weight3 * (velocity[0] + forcing[0]), diffmat, 0, True)
    running = running + derive(weight3 * (velocity[1] + forcing[1]), diffmat, 1, True)
    running = running + derive(weight3 * (velocity[2] + forcing[2]), diffmat, 2, True)
    rhs = assemble(running)

    def weighted(first_vec, second_vec):
        return jnp.sum(first_vec * second_vec * inv_mult)

    pressure = jnp.zeros_like(rhs)
    residual = rhs
    direction = rhs
    local = local_operator(residual, weight3, metric, diffmat)
    partial = jnp.stack([weighted(residual, residual), jnp.sum(residual * local)])
    local, partial = lax.optimization_barrier((local, partial))
    sums = mesh_sum(partial)
    norm_now, curvature = sums[0], sums[1]
    searched = assemble(local)
    step_len = norm_now / curvature
    for iteration in range(1, ITERS + 1):
        pressure = pressure + step_len * direction
        residual = residual - step_len * searched
        if iteration == ITERS:
            break
        local = local_operator(residual, weight3, metric, diffmat)
        partial = jnp.stack(
            [
                weighted(residual, residual),
                jnp.sum(residual * local),
                weighted(residual, searched),
            ]
        )
        local, partial = lax.optimization_barrier((local, partial))
        sums = mesh_sum(partial)
        applied = assemble(local)
        norm_next, own_curvature, cross = sums[0], sums[1], sums[2]
        ratio = norm_next / norm_now
        direction = residual + ratio * direction
        searched = applied + ratio * searched
        curvature = own_curvature + 2.0 * ratio * cross + ratio * ratio * curvature
        norm_now = norm_next
        step_len = norm_now / curvature
    return (pressure, residual)


def solution(mesh):
    return jax.shard_map(
        on_device,
        mesh=mesh,
        in_specs=(
            P(None, "stream", "span", None),
            P("stream", "span", None),
            P(None, ("stream", "span")),
            P(None, ("stream", "span")),
            P(("stream", "span")),
            P(),
            P(("stream", "span"), None),
            P(("stream", "span")),
        ),
        out_specs=(P("stream", "span", None), P("stream", "span", None)),
        check_vma=False,
    )
```

```python
import jax
import jax.numpy as jnp
from jax import lax
from jax.sharding import PartitionSpec as P

POLY = 8
ITERS = 3


kernel_width = 0.45
gll_nodes = [
    -1.0,
    -0.8717401485096066,
    -0.5917001814331423,
    -0.2092992179024789,
    0.2092992179024789,
    0.5917001814331423,
    0.8717401485096066,
    1.0,
]


def with_halo(x, sides, width):
    for axis, dim in sides:
        size, length = (lax.axis_size(axis), x.shape[dim])
        up = [(i, (i + 1) % size) for i in range(size - 1)]
        down = [(j, i) for i, j in up]
        last = lax.slice_in_dim(x, length - width, length, axis=dim)
        first = lax.slice_in_dim(x, 0, width, axis=dim)
        before = lax.ppermute(last, axis, up)
        after = lax.ppermute(first, axis, down)
        x = jnp.concatenate([before, x, after], axis=dim)
    return x


def legendre_value(point, degree):
    previous = 1.0
    current = point
    for order in range(1, degree):
        following = ((2 * order + 1) * point * current - order * previous) / (order + 1)
        previous = current
        current = following
    return current


def gll_tables():
    degree = POLY - 1
    values = [legendre_value(point, degree) for point in gll_nodes]
    weights = [2.0 / (degree * (degree + 1) * value * value) for value in values]
    diffmat = []
    for row_at in range(POLY):
        row_list = []
        for col_at in range(POLY):
            if row_at != col_at:
                row_list.append(
                    values[row_at] / (values[col_at] * (gll_nodes[row_at] - gll_nodes[col_at]))
                )
            elif row_at == 0:
                row_list.append(-degree * (degree + 1) / 4.0)
            elif row_at == degree:
                row_list.append(degree * (degree + 1) / 4.0)
            else:
                row_list.append(0.0)
        diffmat.append(row_list)
    return (
        jnp.asarray(gll_nodes, dtype=jnp.float32),
        jnp.asarray(weights, dtype=jnp.float32),
        jnp.asarray(diffmat, dtype=jnp.float32),
    )


def derive(grid_field, diffmat, axis_at, flipped):
    matrix = diffmat.T if flipped else diffmat
    extent0, extent1, extent2 = grid_field.shape
    highest = lax.Precision.HIGHEST
    if axis_at == 0:
        blocks = grid_field.reshape(extent0 // POLY, POLY, extent1, extent2)
        result = jnp.einsum("ia,xayz->xiyz", matrix, blocks, precision=highest)
    elif axis_at == 1:
        blocks = grid_field.reshape(extent0, extent1 // POLY, POLY, extent2)
        result = jnp.einsum("ib,xybz->xyiz", matrix, blocks, precision=highest)
    else:
        block_width = 128
        tiled_matrix = jnp.kron(jnp.eye(block_width // POLY, dtype=jnp.float32), matrix)
        blocks = grid_field.reshape(extent0, extent1, extent2 // block_width, block_width)
        result = jnp.einsum("xyzc,ic->xyzi", blocks, tiled_matrix, precision=highest)
    return result.reshape(grid_field.shape)


def face_masks(extent):
    node = lax.iota(jnp.int32, extent) % POLY
    return (node == 0, node == POLY - 1)


def assemble(grid_field):
    extent0, extent1, extent2 = grid_field.shape
    first0, last0 = face_masks(extent0)
    first1, last1 = face_masks(extent1)
    first2, last2 = face_masks(extent2)
    first0, last0 = (first0[:, None, None], last0[:, None, None])
    first1, last1 = (first1[None, :, None], last1[None, :, None])
    first2, last2 = (first2[None, None, :], last2[None, None, :])
    nothing = jnp.zeros_like(grid_field)
    padded = with_halo(grid_field, (("stream", 0),), 1)
    running = (
        grid_field + jnp.where(first0, padded[:-2], nothing) + jnp.where(last0, padded[2:], nothing)
    )
    padded = with_halo(running, (("span", 1),), 1)
    running = (
        running
        + jnp.where(first1, padded[:, :-2], nothing)
        + jnp.where(last1, padded[:, 2:], nothing)
    )
    before = jnp.pad(running, ((0, 0), (0, 0), (1, 0)))[:, :, :-1]
    after = jnp.pad(running, ((0, 0), (0, 0), (0, 1)))[:, :, 1:]
    return running + jnp.where(first2, before, nothing) + jnp.where(last2, after, nothing)


def inverse_multiplicity(extent, offset, whole):
    node = lax.iota(jnp.int32, extent) % POLY
    position = offset + lax.iota(jnp.int32, extent)
    inner_face = (node == 0) & (position > 0) | (node == POLY - 1) & (position < whole - 1)
    return jnp.where(inner_face, 0.5, 1.0).astype(jnp.float32)


def mesh_sum(values):
    axes = ("stream", "span")
    count = lax.axis_size(axes)
    spread = jnp.broadcast_to(values[None], (count,) + values.shape)
    gathered = lax.all_to_all(spread, axes, 0, 0, tiled=True)
    return jnp.sum(gathered, axis=0)


def spread_points(arrived, abscissa, extent0, extent1, extent2):
    elems_y, elems_z = (extent1 // POLY, extent2 // POLY)
    kernels = []
    for dimension in range(3):
        kernels.append(
            jnp.exp(
                -(((abscissa[None, :] - arrived[:, dimension : dimension + 1]) / kernel_width) ** 2)
            )
        )
    element = arrived[:, 6].astype(jnp.int32) - 1
    valid = element >= 0
    elem_x = element // (elems_y * elems_z)
    elem_y = (element // elems_z) % elems_y
    elem_z = element % elems_z
    grid0 = lax.iota(jnp.int32, extent0)
    grid1 = lax.iota(jnp.int32, extent1)
    grid2 = lax.iota(jnp.int32, extent2)
    node0 = jnp.tile(kernels[0], (1, extent0 // POLY))
    node1 = jnp.tile(kernels[1], (1, extent1 // POLY))
    node2 = jnp.tile(kernels[2], (1, extent2 // POLY))
    along0 = jnp.where(elem_x[:, None] == grid0[None, :] // POLY, node0, 0.0)
    along1 = jnp.where(elem_y[:, None] == grid1[None, :] // POLY, node1, 0.0)
    along2 = jnp.where(
        valid[:, None] & (elem_z[:, None] == grid2[None, :] // POLY), node2, 0.0
    )
    left = arrived[:, 3:6][:, :, None, None] * (along0[:, None, :, None] * along1[:, None, None, :])
    return jnp.einsum("pcxy,pz->cxyz", left, along2, precision=lax.Precision.HIGHEST)


def project_points(coords, forces, line_id, line_gain, dest_span, owner_element, abscissa, extents):
    points_dev = coords.shape[1]
    spans = lax.axis_size("span")
    capacity = max(2, 2 * points_dev // spans)
    table_ids = lax.iota(jnp.int32, line_gain.shape[0])
    gains = jnp.sum(
        jnp.where(line_id[:, None] == table_ids[None, :], line_gain[None, :], 0.0), axis=1
    )
    scaled = forces * gains[None, :]
    target = dest_span[:, 0]
    owner_code = (owner_element + 1).astype(jnp.float32)
    payload = jnp.concatenate(
        [coords, scaled, owner_code[None, :], target.astype(jnp.float32)[None, :]], axis=0
    ).T
    order = lax.iota(jnp.int32, points_dev)
    earlier = (target[:, None] == target[None, :]) & (order[None, :] < order[:, None])
    ranks = jnp.sum(earlier.astype(jnp.int32), axis=1)
    slot_at = target * capacity + ranks
    outgoing = jnp.zeros((spans * capacity, 8), jnp.float32).at[slot_at].set(payload)
    outgoing = outgoing.reshape(spans, capacity, 8)
    arrived = lax.all_to_all(outgoing, "span", split_axis=0, concat_axis=0, tiled=True).reshape(
        spans * capacity, 8
    )
    return spread_points(arrived, abscissa, extents[0], extents[1], extents[2])


def local_operator(grid_field, weight3, metric, diffmat):
    running = weight3 * grid_field
    for axis_at in range(3):
        running = running + derive(
            metric * derive(grid_field, diffmat, axis_at, False), diffmat, axis_at, True
        )
    return running


def on_device(velocity, coefficient, coords, forces, line_id, line_gain, dest_span, owner_element):
    abscissa, weights, diffmat = gll_tables()
    extent0, extent1, extent2 = coefficient.shape
    tile_zero = jnp.tile(weights, extent0 // POLY)
    tile_one = jnp.tile(weights, extent1 // POLY)
    tile_two = jnp.tile(weights, extent2 // POLY)
    weight3 = tile_zero[:, None, None] * tile_one[None, :, None] * tile_two[None, None, :]
    metric = weight3 * coefficient
    inv_zero = inverse_multiplicity(
        extent0, lax.axis_index("stream") * extent0, extent0 * lax.axis_size("stream")
    )
    inv_one = inverse_multiplicity(
        extent1, lax.axis_index("span") * extent1, extent1 * lax.axis_size("span")
    )
    inv_two = inverse_multiplicity(extent2, 0, extent2)
    inv_mult = inv_zero[:, None, None] * inv_one[None, :, None] * inv_two[None, None, :]
    forcing = project_points(
        coords,
        forces,
        line_id,
        line_gain,
        dest_span,
        owner_element,
        abscissa,
        (extent0, extent1, extent2),
    )
    running = derive(weight3 * (velocity[0] + forcing[0]), diffmat, 0, True)
    running = running + derive(weight3 * (velocity[1] + forcing[1]), diffmat, 1, True)
    running = running + derive(weight3 * (velocity[2] + forcing[2]), diffmat, 2, True)
    rhs = assemble(running)

    def weighted(first_vec, second_vec):
        return jnp.sum(first_vec * second_vec * inv_mult)

    pressure = jnp.zeros_like(rhs)
    residual = rhs
    direction = rhs
    local = local_operator(residual, weight3, metric, diffmat)
    sums = mesh_sum(jnp.stack([weighted(residual, residual), jnp.sum(residual * local)]))
    norm_now, curvature = sums[0], sums[1]
    searched = assemble(local)
    step_len = norm_now / curvature

    def iterate(_, state):
        pressure, residual, direction, searched, norm_now, curvature, step_len = state
        pressure = pressure + step_len * direction
        residual = residual - step_len * searched
        local = local_operator(residual, weight3, metric, diffmat)
        sums = mesh_sum(
            jnp.stack(
                [
                    weighted(residual, residual),
                    jnp.sum(residual * local),
                    weighted(residual, searched),
                ]
            )
        )
        applied = assemble(local)
        norm_next, own_curvature, cross = sums[0], sums[1], sums[2]
        ratio = norm_next / norm_now
        direction = residual + ratio * direction
        searched = applied + ratio * searched
        curvature = own_curvature + 2.0 * ratio * cross + ratio * ratio * curvature
        step_len = norm_next / curvature
        return (pressure, residual, direction, searched, norm_next, curvature, step_len)

    state = (pressure, residual, direction, searched, norm_now, curvature, step_len)
    state = lax.fori_loop(1, ITERS, iterate, state)
    pressure, residual, direction, searched, norm_now, curvature, step_len = state
    pressure = pressure + step_len * direction
    residual = residual - step_len * searched
    return (pressure, residual)


def solution(mesh):
    return jax.shard_map(
        on_device,
        mesh=mesh,
        in_specs=(
            P(None, "stream", "span", None),
            P("stream", "span", None),
            P(None, ("stream", "span")),
            P(None, ("stream", "span")),
            P(("stream", "span")),
            P(),
            P(("stream", "span"), None),
            P(("stream", "span")),
        ),
        out_specs=(P("stream", "span", None), P("stream", "span", None)),
        check_vma=False,
    )
```

```python
import jax
import jax.numpy as jnp
from jax import lax
from jax.sharding import PartitionSpec as P

POLY = 8
ITERS = 3


kernel_width = 0.45
gll_nodes = [
    -1.0,
    -0.8717401485096066,
    -0.5917001814331423,
    -0.2092992179024789,
    0.2092992179024789,
    0.5917001814331423,
    0.8717401485096066,
    1.0,
]


def with_halo(x, sides, width):
    for axis, dim in sides:
        size, length = (lax.axis_size(axis), x.shape[dim])
        up = [(i, (i + 1) % size) for i in range(size - 1)]
        down = [(j, i) for i, j in up]
        last = lax.slice_in_dim(x, length - width, length, axis=dim)
        first = lax.slice_in_dim(x, 0, width, axis=dim)
        before = lax.ppermute(last, axis, up)
        after = lax.ppermute(first, axis, down)
        x = jnp.concatenate([before, x, after], axis=dim)
    return x


def legendre_value(point, degree):
    previous = 1.0
    current = point
    for order in range(1, degree):
        following = ((2 * order + 1) * point * current - order * previous) / (order + 1)
        previous = current
        current = following
    return current


def gll_tables():
    degree = POLY - 1
    values = [legendre_value(point, degree) for point in gll_nodes]
    weights = [2.0 / (degree * (degree + 1) * value * value) for value in values]
    diffmat = []
    for row_at in range(POLY):
        row_list = []
        for col_at in range(POLY):
            if row_at != col_at:
                row_list.append(
                    values[row_at] / (values[col_at] * (gll_nodes[row_at] - gll_nodes[col_at]))
                )
            elif row_at == 0:
                row_list.append(-degree * (degree + 1) / 4.0)
            elif row_at == degree:
                row_list.append(degree * (degree + 1) / 4.0)
            else:
                row_list.append(0.0)
        diffmat.append(row_list)
    return (
        jnp.asarray(gll_nodes, dtype=jnp.float32),
        jnp.asarray(weights, dtype=jnp.float32),
        jnp.asarray(diffmat, dtype=jnp.float32),
    )


def derive(grid_field, diffmat, axis_at, flipped):
    matrix = diffmat.T if flipped else diffmat
    extent0, extent1, extent2 = grid_field.shape
    highest = lax.Precision.HIGHEST
    if axis_at == 0:
        blocks = grid_field.reshape(extent0 // POLY, POLY, extent1, extent2)
        result = jnp.einsum("ia,xayz->xiyz", matrix, blocks, precision=highest)
    elif axis_at == 1:
        blocks = grid_field.reshape(extent0, extent1 // POLY, POLY, extent2)
        result = jnp.einsum("ib,xybz->xyiz", matrix, blocks, precision=highest)
    else:
        block_width = 128
        tiled_matrix = jnp.kron(jnp.eye(block_width // POLY, dtype=jnp.float32), matrix)
        blocks = grid_field.reshape(extent0, extent1, extent2 // block_width, block_width)
        result = jnp.einsum("xyzc,ic->xyzi", blocks, tiled_matrix, precision=highest)
    return result.reshape(grid_field.shape)


def face_masks(extent):
    node = lax.iota(jnp.int32, extent) % POLY
    return (node == 0, node == POLY - 1)


def assemble(grid_field):
    extent0, extent1, extent2 = grid_field.shape
    first0, last0 = face_masks(extent0)
    first1, last1 = face_masks(extent1)
    first2, last2 = face_masks(extent2)
    first0, last0 = (first0[:, None, None], last0[:, None, None])
    first1, last1 = (first1[None, :, None], last1[None, :, None])
    first2, last2 = (first2[None, None, :], last2[None, None, :])
    nothing = jnp.zeros_like(grid_field)
    padded = with_halo(grid_field, (("stream", 0),), 1)
    running = (
        grid_field + jnp.where(first0, padded[:-2], nothing) + jnp.where(last0, padded[2:], nothing)
    )
    padded = with_halo(running, (("span", 1),), 1)
    running = (
        running
        + jnp.where(first1, padded[:, :-2], nothing)
        + jnp.where(last1, padded[:, 2:], nothing)
    )
    before = jnp.pad(running, ((0, 0), (0, 0), (1, 0)))[:, :, :-1]
    after = jnp.pad(running, ((0, 0), (0, 0), (0, 1)))[:, :, 1:]
    return running + jnp.where(first2, before, nothing) + jnp.where(last2, after, nothing)


def inverse_multiplicity(extent, offset, whole):
    node = lax.iota(jnp.int32, extent) % POLY
    position = offset + lax.iota(jnp.int32, extent)
    inner_face = (node == 0) & (position > 0) | (node == POLY - 1) & (position < whole - 1)
    return jnp.where(inner_face, 0.5, 1.0).astype(jnp.float32)


def mesh_sum(values):
    axes = ("stream", "span")
    count = lax.axis_size(axes)
    spread = jnp.broadcast_to(values[None], (count,) + values.shape)
    gathered = lax.all_to_all(spread, axes, 0, 0, tiled=True)
    return jnp.sum(gathered, axis=0)


def along_blocks(factor, matrix):
    points, extent = factor.shape
    blocks = factor.reshape(points, extent // POLY, POLY)
    result = jnp.einsum("pea,ia->pei", blocks, matrix, precision=lax.Precision.HIGHEST)
    return result.reshape(points, extent)


def spread_points(arrived, abscissa, weights, diffmat, extent0, extent1, extent2):
    elems_y, elems_z = (extent1 // POLY, extent2 // POLY)
    kernels = []
    for dimension in range(3):
        kernels.append(
            jnp.exp(
                -(((abscissa[None, :] - arrived[:, dimension : dimension + 1]) / kernel_width) ** 2)
            )
        )
    element = arrived[:, 6].astype(jnp.int32) - 1
    valid = element >= 0
    elem_x = element // (elems_y * elems_z)
    elem_y = (element // elems_z) % elems_y
    elem_z = element % elems_z
    grid0 = lax.iota(jnp.int32, extent0)
    grid1 = lax.iota(jnp.int32, extent1)
    grid2 = lax.iota(jnp.int32, extent2)
    node0 = jnp.tile(kernels[0] * weights[None, :], (1, extent0 // POLY))
    node1 = jnp.tile(kernels[1] * weights[None, :], (1, extent1 // POLY))
    node2 = jnp.tile(kernels[2] * weights[None, :], (1, extent2 // POLY))
    along0 = jnp.where(elem_x[:, None] == grid0[None, :] // POLY, node0, 0.0)
    along1 = jnp.where(elem_y[:, None] == grid1[None, :] // POLY, node1, 0.0)
    along2 = jnp.where(
        valid[:, None] & (elem_z[:, None] == grid2[None, :] // POLY), node2, 0.0
    )
    flipped = diffmat.T
    firsts = jnp.stack([along_blocks(along0, flipped), along0, along0])
    seconds = jnp.stack([along1, along_blocks(along1, flipped), along1])
    thirds = jnp.stack([along2, along2, along_blocks(along2, flipped)])
    scaled = arrived[:, 3:6].T
    left = scaled[:, :, None, None] * (firsts[:, :, :, None] * seconds[:, :, None, :])
    return jnp.einsum("kpxy,kpz->xyz", left, thirds, precision=lax.Precision.HIGHEST)


def project_points(
    coords, forces, line_id, line_gain, dest_span, owner_element, abscissa, weights, diffmat, extents
):
    points_dev = coords.shape[1]
    spans = lax.axis_size("span")
    capacity = max(2, 2 * points_dev // spans)
    table_ids = lax.iota(jnp.int32, line_gain.shape[0])
    gains = jnp.sum(
        jnp.where(line_id[:, None] == table_ids[None, :], line_gain[None, :], 0.0), axis=1
    )
    scaled = forces * gains[None, :]
    target = dest_span[:, 0]
    owner_code = (owner_element + 1).astype(jnp.float32)
    payload = jnp.concatenate(
        [coords, scaled, owner_code[None, :], target.astype(jnp.float32)[None, :]], axis=0
    ).T
    order = lax.iota(jnp.int32, points_dev)
    earlier = (target[:, None] == target[None, :]) & (order[None, :] < order[:, None])
    ranks = jnp.sum(earlier.astype(jnp.int32), axis=1)
    slot_at = target * capacity + ranks
    outgoing = jnp.zeros((spans * capacity, 8), jnp.float32).at[slot_at].set(payload)
    outgoing = outgoing.reshape(spans, capacity, 8)
    arrived = lax.all_to_all(outgoing, "span", split_axis=0, concat_axis=0, tiled=True).reshape(
        spans * capacity, 8
    )
    return spread_points(arrived, abscissa, weights, diffmat, extents[0], extents[1], extents[2])


def local_operator(grid_field, weight3, metric, diffmat):
    running = weight3 * grid_field
    for axis_at in range(3):
        running = running + derive(
            metric * derive(grid_field, diffmat, axis_at, False), diffmat, axis_at, True
        )
    return running


def on_device(velocity, coefficient, coords, forces, line_id, line_gain, dest_span, owner_element):
    abscissa, weights, diffmat = gll_tables()
    extent0, extent1, extent2 = coefficient.shape
    tile_zero = jnp.tile(weights, extent0 // POLY)
    tile_one = jnp.tile(weights, extent1 // POLY)
    tile_two = jnp.tile(weights, extent2 // POLY)
    weight3 = tile_zero[:, None, None] * tile_one[None, :, None] * tile_two[None, None, :]
    metric = weight3 * coefficient
    inv_zero = inverse_multiplicity(
        extent0, lax.axis_index("stream") * extent0, extent0 * lax.axis_size("stream")
    )
    inv_one = inverse_multiplicity(
        extent1, lax.axis_index("span") * extent1, extent1 * lax.axis_size("span")
    )
    inv_two = inverse_multiplicity(extent2, 0, extent2)
    inv_mult = inv_zero[:, None, None] * inv_one[None, :, None] * inv_two[None, None, :]
    forced = project_points(
        coords,
        forces,
        line_id,
        line_gain,
        dest_span,
        owner_element,
        abscissa,
        weights,
        diffmat,
        (extent0, extent1, extent2),
    )
    running = derive(weight3 * velocity[0], diffmat, 0, True)
    running = running + derive(weight3 * velocity[1], diffmat, 1, True)
    running = running + derive(weight3 * velocity[2], diffmat, 2, True)
    rhs = assemble(running + forced)

    def weighted(first_vec, second_vec):
        return jnp.sum(first_vec * second_vec * inv_mult)

    pressure = jnp.zeros_like(rhs)
    residual = rhs
    direction = rhs
    local = local_operator(residual, weight3, metric, diffmat)
    sums = mesh_sum(jnp.stack([weighted(residual, residual), jnp.sum(residual * local)]))
    norm_now, curvature = sums[0], sums[1]
    searched = assemble(local)
    step_len = norm_now / curvature
    for iteration in range(1, ITERS + 1):
        pressure = pressure + step_len * direction
        residual = residual - step_len * searched
        if iteration == ITERS:
            break
        local = local_operator(residual, weight3, metric, diffmat)
        sums = mesh_sum(
            jnp.stack(
                [
                    weighted(residual, residual),
                    jnp.sum(residual * local),
                    weighted(residual, searched),
                ]
            )
        )
        applied = assemble(local)
        norm_next, own_curvature, cross = sums[0], sums[1], sums[2]
        ratio = norm_next / norm_now
        direction = residual + ratio * direction
        searched = applied + ratio * searched
        curvature = own_curvature + 2.0 * ratio * cross + ratio * ratio * curvature
        norm_now = norm_next
        step_len = norm_now / curvature
    return (pressure, residual)


def solution(mesh):
    return jax.shard_map(
        on_device,
        mesh=mesh,
        in_specs=(
            P(None, "stream", "span", None),
            P("stream", "span", None),
            P(None, ("stream", "span")),
            P(None, ("stream", "span")),
            P(("stream", "span")),
            P(),
            P(("stream", "span"), None),
            P(("stream", "span")),
        ),
        out_specs=(P("stream", "span", None), P("stream", "span", None)),
        check_vma=False,
    )
```

```python
import jax
import jax.numpy as jnp
from jax import lax
from jax.sharding import PartitionSpec as P

POLY = 8
ITERS = 3


kernel_width = 0.45
gll_nodes = [
    -1.0,
    -0.8717401485096066,
    -0.5917001814331423,
    -0.2092992179024789,
    0.2092992179024789,
    0.5917001814331423,
    0.8717401485096066,
    1.0,
]


def with_halo(x, sides, width):
    for axis, dim in sides:
        size, length = (lax.axis_size(axis), x.shape[dim])
        up = [(i, (i + 1) % size) for i in range(size - 1)]
        down = [(j, i) for i, j in up]
        last = lax.slice_in_dim(x, length - width, length, axis=dim)
        first = lax.slice_in_dim(x, 0, width, axis=dim)
        before = lax.ppermute(last, axis, up)
        after = lax.ppermute(first, axis, down)
        x = jnp.concatenate([before, x, after], axis=dim)
    return x


def legendre_value(point, degree):
    previous = 1.0
    current = point
    for order in range(1, degree):
        following = ((2 * order + 1) * point * current - order * previous) / (order + 1)
        previous = current
        current = following
    return current


def gll_tables():
    degree = POLY - 1
    values = [legendre_value(point, degree) for point in gll_nodes]
    weights = [2.0 / (degree * (degree + 1) * value * value) for value in values]
    diffmat = []
    for row_at in range(POLY):
        row_list = []
        for col_at in range(POLY):
            if row_at != col_at:
                row_list.append(
                    values[row_at] / (values[col_at] * (gll_nodes[row_at] - gll_nodes[col_at]))
                )
            elif row_at == 0:
                row_list.append(-degree * (degree + 1) / 4.0)
            elif row_at == degree:
                row_list.append(degree * (degree + 1) / 4.0)
            else:
                row_list.append(0.0)
        diffmat.append(row_list)
    return (
        jnp.asarray(gll_nodes, dtype=jnp.float32),
        jnp.asarray(weights, dtype=jnp.float32),
        jnp.asarray(diffmat, dtype=jnp.float32),
    )


def derive(grid_field, diffmat, axis_at, flipped):
    matrix = diffmat.T if flipped else diffmat
    extent0, extent1, extent2 = grid_field.shape
    highest = lax.Precision.HIGHEST
    if axis_at == 0:
        blocks = grid_field.reshape(extent0 // POLY, POLY, extent1, extent2)
        result = jnp.einsum("ia,xayz->xiyz", matrix, blocks, precision=highest)
    elif axis_at == 1:
        blocks = grid_field.reshape(extent0, extent1 // POLY, POLY, extent2)
        result = jnp.einsum("ib,xybz->xyiz", matrix, blocks, precision=highest)
    else:
        block_width = 128
        tiled_matrix = jnp.kron(jnp.eye(block_width // POLY, dtype=jnp.float32), matrix)
        blocks = grid_field.reshape(extent0, extent1, extent2 // block_width, block_width)
        result = jnp.einsum("xyzc,ic->xyzi", blocks, tiled_matrix, precision=highest)
    return result.reshape(grid_field.shape)


def face_masks(extent):
    node = lax.iota(jnp.int32, extent) % POLY
    return (node == 0, node == POLY - 1)


def assemble(grid_field):
    extent0, extent1, extent2 = grid_field.shape
    first0, last0 = face_masks(extent0)
    first1, last1 = face_masks(extent1)
    first2, last2 = face_masks(extent2)
    first0, last0 = (first0[:, None, None], last0[:, None, None])
    first1, last1 = (first1[None, :, None], last1[None, :, None])
    first2, last2 = (first2[None, None, :], last2[None, None, :])
    nothing = jnp.zeros_like(grid_field)
    padded = with_halo(grid_field, (("stream", 0),), 1)
    running = (
        grid_field + jnp.where(first0, padded[:-2], nothing) + jnp.where(last0, padded[2:], nothing)
    )
    padded = with_halo(running, (("span", 1),), 1)
    running = (
        running
        + jnp.where(first1, padded[:, :-2], nothing)
        + jnp.where(last1, padded[:, 2:], nothing)
    )
    before = jnp.pad(running, ((0, 0), (0, 0), (1, 0)))[:, :, :-1]
    after = jnp.pad(running, ((0, 0), (0, 0), (0, 1)))[:, :, 1:]
    return running + jnp.where(first2, before, nothing) + jnp.where(last2, after, nothing)


def assemble_span_first(grid_field):
    extent0, extent1, extent2 = grid_field.shape
    first0, last0 = face_masks(extent0)
    first1, last1 = face_masks(extent1)
    first2, last2 = face_masks(extent2)
    first0, last0 = (first0[:, None, None], last0[:, None, None])
    first1, last1 = (first1[None, :, None], last1[None, :, None])
    first2, last2 = (first2[None, None, :], last2[None, None, :])
    nothing = jnp.zeros_like(grid_field)
    padded = with_halo(grid_field, (("span", 1),), 1)
    running = (
        grid_field
        + jnp.where(first1, padded[:, :-2], nothing)
        + jnp.where(last1, padded[:, 2:], nothing)
    )
    padded = with_halo(running, (("stream", 0),), 1)
    running = running + jnp.where(first0, padded[:-2], nothing) + jnp.where(last0, padded[2:], nothing)
    before = jnp.pad(running, ((0, 0), (0, 0), (1, 0)))[:, :, :-1]
    after = jnp.pad(running, ((0, 0), (0, 0), (0, 1)))[:, :, 1:]
    return running + jnp.where(first2, before, nothing) + jnp.where(last2, after, nothing)


def inverse_multiplicity(extent, offset, whole):
    node = lax.iota(jnp.int32, extent) % POLY
    position = offset + lax.iota(jnp.int32, extent)
    inner_face = (node == 0) & (position > 0) | (node == POLY - 1) & (position < whole - 1)
    return jnp.where(inner_face, 0.5, 1.0).astype(jnp.float32)


def mesh_sum(values):
    axes = ("stream", "span")
    count = lax.axis_size(axes)
    spread = jnp.broadcast_to(values[None], (count,) + values.shape)
    gathered = lax.all_to_all(spread, axes, 0, 0, tiled=True)
    return jnp.sum(gathered, axis=0)


def spread_points(arrived, abscissa, extent0, extent1, extent2):
    elems_y, elems_z = (extent1 // POLY, extent2 // POLY)
    kernels = []
    for dimension in range(3):
        kernels.append(
            jnp.exp(
                -(((abscissa[None, :] - arrived[:, dimension : dimension + 1]) / kernel_width) ** 2)
            )
        )
    element = arrived[:, 6].astype(jnp.int32) - 1
    valid = element >= 0
    elem_x = element // (elems_y * elems_z)
    elem_y = (element // elems_z) % elems_y
    elem_z = element % elems_z
    grid0 = lax.iota(jnp.int32, extent0)
    grid1 = lax.iota(jnp.int32, extent1)
    grid2 = lax.iota(jnp.int32, extent2)
    node0 = jnp.tile(kernels[0], (1, extent0 // POLY))
    node1 = jnp.tile(kernels[1], (1, extent1 // POLY))
    node2 = jnp.tile(kernels[2], (1, extent2 // POLY))
    along0 = jnp.where(elem_x[:, None] == grid0[None, :] // POLY, node0, 0.0)
    along1 = jnp.where(elem_y[:, None] == grid1[None, :] // POLY, node1, 0.0)
    along2 = jnp.where(
        valid[:, None] & (elem_z[:, None] == grid2[None, :] // POLY), node2, 0.0
    )
    left = arrived[:, 3:6][:, :, None, None] * (along0[:, None, :, None] * along1[:, None, None, :])
    return jnp.einsum("pcxy,pz->cxyz", left, along2, precision=lax.Precision.HIGHEST)


def project_points(coords, forces, line_id, line_gain, dest_span, owner_element, abscissa, extents):
    points_dev = coords.shape[1]
    spans = lax.axis_size("span")
    capacity = max(2, 2 * points_dev // spans)
    table_ids = lax.iota(jnp.int32, line_gain.shape[0])
    gains = jnp.sum(
        jnp.where(line_id[:, None] == table_ids[None, :], line_gain[None, :], 0.0), axis=1
    )
    scaled = forces * gains[None, :]
    target = dest_span[:, 0]
    owner_code = (owner_element + 1).astype(jnp.float32)
    payload = jnp.concatenate(
        [coords, scaled, owner_code[None, :], target.astype(jnp.float32)[None, :]], axis=0
    ).T
    order = lax.iota(jnp.int32, points_dev)
    earlier = (target[:, None] == target[None, :]) & (order[None, :] < order[:, None])
    ranks = jnp.sum(earlier.astype(jnp.int32), axis=1)
    slot_at = target * capacity + ranks
    outgoing = jnp.zeros((spans * capacity, 8), jnp.float32).at[slot_at].set(payload)
    outgoing = outgoing.reshape(spans, capacity, 8)
    arrived = lax.all_to_all(outgoing, "span", split_axis=0, concat_axis=0, tiled=True).reshape(
        spans * capacity, 8
    )
    return spread_points(arrived, abscissa, extents[0], extents[1], extents[2])


def local_operator(grid_field, weight3, metric, diffmat):
    running = weight3 * grid_field
    for axis_at in range(3):
        running = running + derive(
            metric * derive(grid_field, diffmat, axis_at, False), diffmat, axis_at, True
        )
    return running


def on_device(velocity, coefficient, coords, forces, line_id, line_gain, dest_span, owner_element):
    abscissa, weights, diffmat = gll_tables()
    extent0, extent1, extent2 = coefficient.shape
    tile_zero = jnp.tile(weights, extent0 // POLY)
    tile_one = jnp.tile(weights, extent1 // POLY)
    tile_two = jnp.tile(weights, extent2 // POLY)
    weight3 = tile_zero[:, None, None] * tile_one[None, :, None] * tile_two[None, None, :]
    metric = weight3 * coefficient
    inv_zero = inverse_multiplicity(
        extent0, lax.axis_index("stream") * extent0, extent0 * lax.axis_size("stream")
    )
    inv_one = inverse_multiplicity(
        extent1, lax.axis_index("span") * extent1, extent1 * lax.axis_size("span")
    )
    inv_two = inverse_multiplicity(extent2, 0, extent2)
    inv_mult = inv_zero[:, None, None] * inv_one[None, :, None] * inv_two[None, None, :]
    forcing = project_points(
        coords,
        forces,
        line_id,
        line_gain,
        dest_span,
        owner_element,
        abscissa,
        (extent0, extent1, extent2),
    )
    running = derive(weight3 * (velocity[0] + forcing[0]), diffmat, 0, True)
    running = running + derive(weight3 * (velocity[1] + forcing[1]), diffmat, 1, True)
    running = running + derive(weight3 * (velocity[2] + forcing[2]), diffmat, 2, True)
    rhs = assemble(running)

    def weighted(first_vec, second_vec):
        return jnp.sum(first_vec * second_vec * inv_mult)

    pressure = jnp.zeros_like(rhs)
    residual = rhs
    direction = rhs
    local = local_operator(residual, weight3, metric, diffmat)
    sums = mesh_sum(jnp.stack([weighted(residual, residual), jnp.sum(residual * local)]))
    norm_now, curvature = sums[0], sums[1]
    searched = assemble_span_first(local)
    step_len = norm_now / curvature
    for iteration in range(1, ITERS + 1):
        pressure = pressure + step_len * direction
        residual = residual - step_len * searched
        if iteration == ITERS:
            break
        local = local_operator(residual, weight3, metric, diffmat)
        sums = mesh_sum(
            jnp.stack(
                [
                    weighted(residual, residual),
                    jnp.sum(residual * local),
                    weighted(residual, searched),
                ]
            )
        )
        applied = assemble_span_first(local)
        norm_next, own_curvature, cross = sums[0], sums[1], sums[2]
        ratio = norm_next / norm_now
        direction = residual + ratio * direction
        searched = applied + ratio * searched
        curvature = own_curvature + 2.0 * ratio * cross + ratio * ratio * curvature
        norm_now = norm_next
        step_len = norm_now / curvature
    return (pressure, residual)


def solution(mesh):
    return jax.shard_map(
        on_device,
        mesh=mesh,
        in_specs=(
            P(None, "stream", "span", None),
            P("stream", "span", None),
            P(None, ("stream", "span")),
            P(None, ("stream", "span")),
            P(("stream", "span")),
            P(),
            P(("stream", "span"), None),
            P(("stream", "span")),
        ),
        out_specs=(P("stream", "span", None), P("stream", "span", None)),
        check_vma=False,
    )
```

```python
import jax
import jax.numpy as jnp
from jax import lax
from jax.sharding import PartitionSpec as P

POLY = 8
ITERS = 3


kernel_width = 0.45
gll_nodes = [
    -1.0,
    -0.8717401485096066,
    -0.5917001814331423,
    -0.2092992179024789,
    0.2092992179024789,
    0.5917001814331423,
    0.8717401485096066,
    1.0,
]


def with_halo(x, sides, width):
    for axis, dim in sides:
        size, length = (lax.axis_size(axis), x.shape[dim])
        up = [(i, (i + 1) % size) for i in range(size - 1)]
        down = [(j, i) for i, j in up]
        last = lax.slice_in_dim(x, length - width, length, axis=dim)
        first = lax.slice_in_dim(x, 0, width, axis=dim)
        before = lax.ppermute(last, axis, up)
        after = lax.ppermute(first, axis, down)
        x = jnp.concatenate([before, x, after], axis=dim)
    return x


def legendre_value(point, degree):
    previous = 1.0
    current = point
    for order in range(1, degree):
        following = ((2 * order + 1) * point * current - order * previous) / (order + 1)
        previous = current
        current = following
    return current


def gll_tables():
    degree = POLY - 1
    values = [legendre_value(point, degree) for point in gll_nodes]
    weights = [2.0 / (degree * (degree + 1) * value * value) for value in values]
    diffmat = []
    for row_at in range(POLY):
        row_list = []
        for col_at in range(POLY):
            if row_at != col_at:
                row_list.append(
                    values[row_at] / (values[col_at] * (gll_nodes[row_at] - gll_nodes[col_at]))
                )
            elif row_at == 0:
                row_list.append(-degree * (degree + 1) / 4.0)
            elif row_at == degree:
                row_list.append(degree * (degree + 1) / 4.0)
            else:
                row_list.append(0.0)
        diffmat.append(row_list)
    return (
        jnp.asarray(gll_nodes, dtype=jnp.float32),
        jnp.asarray(weights, dtype=jnp.float32),
        jnp.asarray(diffmat, dtype=jnp.float32),
    )


def derive(grid_field, diffmat, axis_at, flipped):
    matrix = diffmat.T if flipped else diffmat
    extent0, extent1, extent2 = grid_field.shape
    highest = lax.Precision.HIGHEST
    if axis_at == 0:
        blocks = grid_field.reshape(extent0 // POLY, POLY, extent1, extent2)
        result = jnp.einsum("ia,xayz->xiyz", matrix, blocks, precision=highest)
    elif axis_at == 1:
        blocks = grid_field.reshape(extent0, extent1 // POLY, POLY, extent2)
        result = jnp.einsum("ib,xybz->xyiz", matrix, blocks, precision=highest)
    else:
        block_width = 128
        tiled_matrix = jnp.kron(jnp.eye(block_width // POLY, dtype=jnp.float32), matrix)
        blocks = grid_field.reshape(extent0, extent1, extent2 // block_width, block_width)
        result = jnp.einsum("xyzc,ic->xyzi", blocks, tiled_matrix, precision=highest)
    return result.reshape(grid_field.shape)


def face_masks(extent):
    node = lax.iota(jnp.int32, extent) % POLY
    return (node == 0, node == POLY - 1)


def assemble(grid_field):
    extent0, extent1, extent2 = grid_field.shape
    first0, last0 = face_masks(extent0)
    first1, last1 = face_masks(extent1)
    first2, last2 = face_masks(extent2)
    first0, last0 = (first0[:, None, None], last0[:, None, None])
    first1, last1 = (first1[None, :, None], last1[None, :, None])
    first2, last2 = (first2[None, None, :], last2[None, None, :])
    nothing = jnp.zeros_like(grid_field)
    padded = with_halo(grid_field, (("stream", 0),), 1)
    running = (
        grid_field + jnp.where(first0, padded[:-2], nothing) + jnp.where(last0, padded[2:], nothing)
    )
    padded = with_halo(running, (("span", 1),), 1)
    running = (
        running
        + jnp.where(first1, padded[:, :-2], nothing)
        + jnp.where(last1, padded[:, 2:], nothing)
    )
    before = jnp.pad(running, ((0, 0), (0, 0), (1, 0)))[:, :, :-1]
    after = jnp.pad(running, ((0, 0), (0, 0), (0, 1)))[:, :, 1:]
    return running + jnp.where(first2, before, nothing) + jnp.where(last2, after, nothing)


def inverse_multiplicity(extent, offset, whole):
    node = lax.iota(jnp.int32, extent) % POLY
    position = offset + lax.iota(jnp.int32, extent)
    inner_face = (node == 0) & (position > 0) | (node == POLY - 1) & (position < whole - 1)
    return jnp.where(inner_face, 0.5, 1.0).astype(jnp.float32)


def mesh_sum(values):
    axes = ("stream", "span")
    count = lax.axis_size(axes)
    spread = jnp.broadcast_to(values[None], (count,) + values.shape)
    gathered = lax.all_to_all(spread, axes, 0, 0, tiled=True)
    return jnp.sum(gathered, axis=0)


def spread_points(arrived, abscissa, extent0, extent1, extent2):
    elems_y, elems_z = (extent1 // POLY, extent2 // POLY)
    kernels = []
    for dimension in range(3):
        kernels.append(
            jnp.exp(
                -(((abscissa[None, :] - arrived[:, dimension : dimension + 1]) / kernel_width) ** 2)
            )
        )
    element = arrived[:, 6].astype(jnp.int32) - 1
    valid = element >= 0
    elem_x = element // (elems_y * elems_z)
    elem_y = (element // elems_z) % elems_y
    elem_z = element % elems_z
    grid0 = lax.iota(jnp.int32, extent0)
    grid1 = lax.iota(jnp.int32, extent1)
    grid2 = lax.iota(jnp.int32, extent2)
    node0 = jnp.tile(kernels[0], (1, extent0 // POLY))
    node1 = jnp.tile(kernels[1], (1, extent1 // POLY))
    node2 = jnp.tile(kernels[2], (1, extent2 // POLY))
    along0 = jnp.where(elem_x[:, None] == grid0[None, :] // POLY, node0, 0.0)
    along1 = jnp.where(elem_y[:, None] == grid1[None, :] // POLY, node1, 0.0)
    along2 = jnp.where(
        valid[:, None] & (elem_z[:, None] == grid2[None, :] // POLY), node2, 0.0
    )
    left = arrived[:, 3:6][:, :, None, None] * (along0[:, None, :, None] * along1[:, None, None, :])
    return jnp.einsum("pcxy,pz->cxyz", left, along2, precision=lax.Precision.HIGHEST)


def project_points(coords, forces, line_id, line_gain, dest_span, owner_element, abscissa, extents):
    points_dev = coords.shape[1]
    spans = lax.axis_size("span")
    capacity = max(2, 2 * points_dev // spans)
    table_ids = lax.iota(jnp.int32, line_gain.shape[0])
    gains = jnp.sum(
        jnp.where(line_id[:, None] == table_ids[None, :], line_gain[None, :], 0.0), axis=1
    )
    scaled = forces * gains[None, :]
    target = dest_span[:, 0]
    owner_code = (owner_element + 1).astype(jnp.float32)
    payload = jnp.concatenate(
        [coords, scaled, owner_code[None, :], target.astype(jnp.float32)[None, :]], axis=0
    ).T
    order = lax.iota(jnp.int32, points_dev)
    earlier = (target[:, None] == target[None, :]) & (order[None, :] < order[:, None])
    ranks = jnp.sum(earlier.astype(jnp.int32), axis=1)
    slot_at = target * capacity + ranks
    outgoing = jnp.zeros((spans * capacity, 8), jnp.float32).at[slot_at].set(payload)
    outgoing = outgoing.reshape(spans, capacity, 8)
    arrived = lax.all_to_all(outgoing, "span", split_axis=0, concat_axis=0, tiled=True).reshape(
        spans * capacity, 8
    )
    return spread_points(arrived, abscissa, extents[0], extents[1], extents[2])


def local_operator(grid_field, weight3, metric, diffmat):
    running = weight3 * grid_field
    for axis_at in range(3):
        running = running + derive(
            metric * derive(grid_field, diffmat, axis_at, False), diffmat, axis_at, True
        )
    return running


def on_device(velocity, coefficient, coords, forces, line_id, line_gain, dest_span, owner_element):
    abscissa, weights, diffmat = gll_tables()
    extent0, extent1, extent2 = coefficient.shape
    tile_zero = jnp.tile(weights, extent0 // POLY)
    tile_one = jnp.tile(weights, extent1 // POLY)
    tile_two = jnp.tile(weights, extent2 // POLY)
    weight3 = tile_zero[:, None, None] * tile_one[None, :, None] * tile_two[None, None, :]
    metric = weight3 * coefficient
    inv_zero = inverse_multiplicity(
        extent0, lax.axis_index("stream") * extent0, extent0 * lax.axis_size("stream")
    )
    inv_one = inverse_multiplicity(
        extent1, lax.axis_index("span") * extent1, extent1 * lax.axis_size("span")
    )
    inv_two = inverse_multiplicity(extent2, 0, extent2)
    inv_mult = inv_zero[:, None, None] * inv_one[None, :, None] * inv_two[None, None, :]
    forcing = project_points(
        coords,
        forces,
        line_id,
        line_gain,
        dest_span,
        owner_element,
        abscissa,
        (extent0, extent1, extent2),
    )
    running = derive(weight3 * (velocity[0] + forcing[0]), diffmat, 0, True)
    running = running + derive(weight3 * (velocity[1] + forcing[1]), diffmat, 1, True)
    running = running + derive(weight3 * (velocity[2] + forcing[2]), diffmat, 2, True)
    rhs = assemble(running)

    pressure = jnp.zeros_like(rhs)
    residual = rhs
    direction = rhs
    local = local_operator(residual, weight3, metric, diffmat)
    terms = jnp.stack([residual * residual * inv_mult, residual * local])
    sums = mesh_sum(jnp.sum(terms, axis=(1, 2, 3)))
    norm_now, curvature = sums[0], sums[1]
    searched = assemble(local)
    step_len = norm_now / curvature
    for iteration in range(1, ITERS + 1):
        pressure = pressure + step_len * direction
        residual = residual - step_len * searched
        if iteration == ITERS:
            break
        local = local_operator(residual, weight3, metric, diffmat)
        terms = jnp.stack(
            [residual * residual * inv_mult, residual * local, residual * searched * inv_mult]
        )
        sums = mesh_sum(jnp.sum(terms, axis=(1, 2, 3)))
        applied = assemble(local)
        norm_next, own_curvature, cross = sums[0], sums[1], sums[2]
        ratio = norm_next / norm_now
        direction = residual + ratio * direction
        searched = applied + ratio * searched
        curvature = own_curvature + 2.0 * ratio * cross + ratio * ratio * curvature
        norm_now = norm_next
        step_len = norm_now / curvature
    return (pressure, residual)


def solution(mesh):
    return jax.shard_map(
        on_device,
        mesh=mesh,
        in_specs=(
            P(None, "stream", "span", None),
            P("stream", "span", None),
            P(None, ("stream", "span")),
            P(None, ("stream", "span")),
            P(("stream", "span")),
            P(),
            P(("stream", "span"), None),
            P(("stream", "span")),
        ),
        out_specs=(P("stream", "span", None), P("stream", "span", None)),
        check_vma=False,
    )
```

```python
import jax
import jax.numpy as jnp
from jax import lax
from jax.sharding import PartitionSpec as P

POLY = 8
ITERS = 3


kernel_width = 0.45
gll_nodes = [
    -1.0,
    -0.8717401485096066,
    -0.5917001814331423,
    -0.2092992179024789,
    0.2092992179024789,
    0.5917001814331423,
    0.8717401485096066,
    1.0,
]


def with_halo(x, sides, width):
    for axis, dim in sides:
        size, length = (lax.axis_size(axis), x.shape[dim])
        up = [(i, (i + 1) % size) for i in range(size - 1)]
        down = [(j, i) for i, j in up]
        last = lax.slice_in_dim(x, length - width, length, axis=dim)
        first = lax.slice_in_dim(x, 0, width, axis=dim)
        before = lax.ppermute(last, axis, up)
        after = lax.ppermute(first, axis, down)
        x = jnp.concatenate([before, x, after], axis=dim)
    return x


def legendre_value(point, degree):
    previous = 1.0
    current = point
    for order in range(1, degree):
        following = ((2 * order + 1) * point * current - order * previous) / (order + 1)
        previous = current
        current = following
    return current


def gll_tables():
    degree = POLY - 1
    values = [legendre_value(point, degree) for point in gll_nodes]
    weights = [2.0 / (degree * (degree + 1) * value * value) for value in values]
    diffmat = []
    for row_at in range(POLY):
        row_list = []
        for col_at in range(POLY):
            if row_at != col_at:
                row_list.append(
                    values[row_at] / (values[col_at] * (gll_nodes[row_at] - gll_nodes[col_at]))
                )
            elif row_at == 0:
                row_list.append(-degree * (degree + 1) / 4.0)
            elif row_at == degree:
                row_list.append(degree * (degree + 1) / 4.0)
            else:
                row_list.append(0.0)
        diffmat.append(row_list)
    return (
        jnp.asarray(gll_nodes, dtype=jnp.float32),
        jnp.asarray(weights, dtype=jnp.float32),
        jnp.asarray(diffmat, dtype=jnp.float32),
    )


def derive(grid_field, diffmat, axis_at, flipped):
    matrix = diffmat.T if flipped else diffmat
    extent0, extent1, extent2 = grid_field.shape
    highest = lax.Precision.HIGHEST
    if axis_at == 0:
        blocks = grid_field.reshape(extent0 // POLY, POLY, extent1, extent2)
        result = jnp.einsum("ia,xayz->xiyz", matrix, blocks, precision=highest)
    elif axis_at == 1:
        tiled_matrix = jnp.kron(jnp.eye(extent1 // POLY, dtype=jnp.float32), matrix)
        result = jnp.einsum("ib,xbz->xiz", tiled_matrix, grid_field, precision=highest)
    else:
        block_width = 128
        tiled_matrix = jnp.kron(jnp.eye(block_width // POLY, dtype=jnp.float32), matrix)
        blocks = grid_field.reshape(extent0, extent1, extent2 // block_width, block_width)
        result = jnp.einsum("xyzc,ic->xyzi", blocks, tiled_matrix, precision=highest)
    return result.reshape(grid_field.shape)


def face_masks(extent):
    node = lax.iota(jnp.int32, extent) % POLY
    return (node == 0, node == POLY - 1)


def assemble(grid_field):
    extent0, extent1, extent2 = grid_field.shape
    first0, last0 = face_masks(extent0)
    first1, last1 = face_masks(extent1)
    first2, last2 = face_masks(extent2)
    first0, last0 = (first0[:, None, None], last0[:, None, None])
    first1, last1 = (first1[None, :, None], last1[None, :, None])
    first2, last2 = (first2[None, None, :], last2[None, None, :])
    nothing = jnp.zeros_like(grid_field)
    padded = with_halo(grid_field, (("stream", 0),), 1)
    running = (
        grid_field + jnp.where(first0, padded[:-2], nothing) + jnp.where(last0, padded[2:], nothing)
    )
    padded = with_halo(running, (("span", 1),), 1)
    running = (
        running
        + jnp.where(first1, padded[:, :-2], nothing)
        + jnp.where(last1, padded[:, 2:], nothing)
    )
    before = jnp.pad(running, ((0, 0), (0, 0), (1, 0)))[:, :, :-1]
    after = jnp.pad(running, ((0, 0), (0, 0), (0, 1)))[:, :, 1:]
    return running + jnp.where(first2, before, nothing) + jnp.where(last2, after, nothing)


def inverse_multiplicity(extent, offset, whole):
    node = lax.iota(jnp.int32, extent) % POLY
    position = offset + lax.iota(jnp.int32, extent)
    inner_face = (node == 0) & (position > 0) | (node == POLY - 1) & (position < whole - 1)
    return jnp.where(inner_face, 0.5, 1.0).astype(jnp.float32)


def mesh_sum(values):
    axes = ("stream", "span")
    count = lax.axis_size(axes)
    spread = jnp.broadcast_to(values[None], (count,) + values.shape)
    gathered = lax.all_to_all(spread, axes, 0, 0, tiled=True)
    return jnp.sum(gathered, axis=0)


def spread_points(arrived, abscissa, extent0, extent1, extent2):
    elems_y, elems_z = (extent1 // POLY, extent2 // POLY)
    kernels = []
    for dimension in range(3):
        kernels.append(
            jnp.exp(
                -(((abscissa[None, :] - arrived[:, dimension : dimension + 1]) / kernel_width) ** 2)
            )
        )
    element = arrived[:, 6].astype(jnp.int32) - 1
    valid = element >= 0
    elem_x = element // (elems_y * elems_z)
    elem_y = (element // elems_z) % elems_y
    elem_z = element % elems_z
    grid0 = lax.iota(jnp.int32, extent0)
    grid1 = lax.iota(jnp.int32, extent1)
    grid2 = lax.iota(jnp.int32, extent2)
    node0 = jnp.tile(kernels[0], (1, extent0 // POLY))
    node1 = jnp.tile(kernels[1], (1, extent1 // POLY))
    node2 = jnp.tile(kernels[2], (1, extent2 // POLY))
    along0 = jnp.where(elem_x[:, None] == grid0[None, :] // POLY, node0, 0.0)
    along1 = jnp.where(elem_y[:, None] == grid1[None, :] // POLY, node1, 0.0)
    along2 = jnp.where(
        valid[:, None] & (elem_z[:, None] == grid2[None, :] // POLY), node2, 0.0
    )
    left = arrived[:, 3:6][:, :, None, None] * (along0[:, None, :, None] * along1[:, None, None, :])
    return jnp.einsum("pcxy,pz->cxyz", left, along2, precision=lax.Precision.HIGHEST)


def project_points(coords, forces, line_id, line_gain, dest_span, owner_element, abscissa, extents):
    points_dev = coords.shape[1]
    spans = lax.axis_size("span")
    capacity = max(2, 2 * points_dev // spans)
    table_ids = lax.iota(jnp.int32, line_gain.shape[0])
    gains = jnp.sum(
        jnp.where(line_id[:, None] == table_ids[None, :], line_gain[None, :], 0.0), axis=1
    )
    scaled = forces * gains[None, :]
    target = dest_span[:, 0]
    owner_code = (owner_element + 1).astype(jnp.float32)
    payload = jnp.concatenate(
        [coords, scaled, owner_code[None, :], target.astype(jnp.float32)[None, :]], axis=0
    ).T
    order = lax.iota(jnp.int32, points_dev)
    earlier = (target[:, None] == target[None, :]) & (order[None, :] < order[:, None])
    ranks = jnp.sum(earlier.astype(jnp.int32), axis=1)
    slot_at = target * capacity + ranks
    outgoing = jnp.zeros((spans * capacity, 8), jnp.float32).at[slot_at].set(payload)
    outgoing = outgoing.reshape(spans, capacity, 8)
    arrived = lax.all_to_all(outgoing, "span", split_axis=0, concat_axis=0, tiled=True).reshape(
        spans * capacity, 8
    )
    return spread_points(arrived, abscissa, extents[0], extents[1], extents[2])


def local_operator(grid_field, weight3, metric, diffmat):
    running = weight3 * grid_field
    for axis_at in range(3):
        running = running + derive(
            metric * derive(grid_field, diffmat, axis_at, False), diffmat, axis_at, True
        )
    return running


def on_device(velocity, coefficient, coords, forces, line_id, line_gain, dest_span, owner_element):
    abscissa, weights, diffmat = gll_tables()
    extent0, extent1, extent2 = coefficient.shape
    tile_zero = jnp.tile(weights, extent0 // POLY)
    tile_one = jnp.tile(weights, extent1 // POLY)
    tile_two = jnp.tile(weights, extent2 // POLY)
    weight3 = tile_zero[:, None, None] * tile_one[None, :, None] * tile_two[None, None, :]
    metric = weight3 * coefficient
    inv_zero = inverse_multiplicity(
        extent0, lax.axis_index("stream") * extent0, extent0 * lax.axis_size("stream")
    )
    inv_one = inverse_multiplicity(
        extent1, lax.axis_index("span") * extent1, extent1 * lax.axis_size("span")
    )
    inv_two = inverse_multiplicity(extent2, 0, extent2)
    inv_mult = inv_zero[:, None, None] * inv_one[None, :, None] * inv_two[None, None, :]
    forcing = project_points(
        coords,
        forces,
        line_id,
        line_gain,
        dest_span,
        owner_element,
        abscissa,
        (extent0, extent1, extent2),
    )
    running = derive(weight3 * (velocity[0] + forcing[0]), diffmat, 0, True)
    running = running + derive(weight3 * (velocity[1] + forcing[1]), diffmat, 1, True)
    running = running + derive(weight3 * (velocity[2] + forcing[2]), diffmat, 2, True)
    rhs = assemble(running)

    pressure = jnp.zeros_like(rhs)
    residual = rhs
    direction = rhs
    local = local_operator(residual, weight3, metric, diffmat)
    terms = jnp.stack([residual * residual * inv_mult, residual * local])
    sums = mesh_sum(jnp.sum(terms, axis=(1, 2, 3)))
    norm_now, curvature = sums[0], sums[1]
    searched = assemble(local)
    step_len = norm_now / curvature
    for iteration in range(1, ITERS + 1):
        pressure = pressure + step_len * direction
        residual = residual - step_len * searched
        if iteration == ITERS:
            break
        local = local_operator(residual, weight3, metric, diffmat)
        terms = jnp.stack(
            [residual * residual * inv_mult, residual * local, residual * searched * inv_mult]
        )
        sums = mesh_sum(jnp.sum(terms, axis=(1, 2, 3)))
        applied = assemble(local)
        norm_next, own_curvature, cross = sums[0], sums[1], sums[2]
        ratio = norm_next / norm_now
        direction = residual + ratio * direction
        searched = applied + ratio * searched
        curvature = own_curvature + 2.0 * ratio * cross + ratio * ratio * curvature
        norm_now = norm_next
        step_len = norm_now / curvature
    return (pressure, residual)


def solution(mesh):
    return jax.shard_map(
        on_device,
        mesh=mesh,
        in_specs=(
            P(None, "stream", "span", None),
            P("stream", "span", None),
            P(None, ("stream", "span")),
            P(None, ("stream", "span")),
            P(("stream", "span")),
            P(),
            P(("stream", "span"), None),
            P(("stream", "span")),
        ),
        out_specs=(P("stream", "span", None), P("stream", "span", None)),
        check_vma=False,
    )
```

```python
import jax
import jax.numpy as jnp
from jax import lax
from jax.sharding import PartitionSpec as P

POLY = 8
ITERS = 3


kernel_width = 0.45
gll_nodes = [
    -1.0,
    -0.8717401485096066,
    -0.5917001814331423,
    -0.2092992179024789,
    0.2092992179024789,
    0.5917001814331423,
    0.8717401485096066,
    1.0,
]


def with_halo(x, sides, width):
    for axis, dim in sides:
        size, length = (lax.axis_size(axis), x.shape[dim])
        up = [(i, (i + 1) % size) for i in range(size - 1)]
        down = [(j, i) for i, j in up]
        last = lax.slice_in_dim(x, length - width, length, axis=dim)
        first = lax.slice_in_dim(x, 0, width, axis=dim)
        before = lax.ppermute(last, axis, up)
        after = lax.ppermute(first, axis, down)
        x = jnp.concatenate([before, x, after], axis=dim)
    return x


def legendre_value(point, degree):
    previous = 1.0
    current = point
    for order in range(1, degree):
        following = ((2 * order + 1) * point * current - order * previous) / (order + 1)
        previous = current
        current = following
    return current


def gll_tables():
    degree = POLY - 1
    values = [legendre_value(point, degree) for point in gll_nodes]
    weights = [2.0 / (degree * (degree + 1) * value * value) for value in values]
    diffmat = []
    for row_at in range(POLY):
        row_list = []
        for col_at in range(POLY):
            if row_at != col_at:
                row_list.append(
                    values[row_at] / (values[col_at] * (gll_nodes[row_at] - gll_nodes[col_at]))
                )
            elif row_at == 0:
                row_list.append(-degree * (degree + 1) / 4.0)
            elif row_at == degree:
                row_list.append(degree * (degree + 1) / 4.0)
            else:
                row_list.append(0.0)
        diffmat.append(row_list)
    return (
        jnp.asarray(gll_nodes, dtype=jnp.float32),
        jnp.asarray(weights, dtype=jnp.float32),
        jnp.asarray(diffmat, dtype=jnp.float32),
    )


def derive(grid_field, diffmat, axis_at, flipped):
    matrix = diffmat.T if flipped else diffmat
    extent0, extent1, extent2 = grid_field.shape
    highest = lax.Precision.HIGHEST
    if axis_at == 0:
        blocks = grid_field.reshape(extent0 // POLY, POLY, extent1, extent2)
        result = jnp.einsum("ia,xayz->xiyz", matrix, blocks, precision=highest)
    elif axis_at == 1:
        tiled_matrix = jnp.kron(jnp.eye(extent1 // POLY, dtype=jnp.float32), matrix)
        result = jnp.einsum("ib,xbz->xiz", tiled_matrix, grid_field, precision=highest)
    else:
        block_width = 128
        tiled_matrix = jnp.kron(jnp.eye(block_width // POLY, dtype=jnp.float32), matrix)
        blocks = grid_field.reshape(extent0, extent1, extent2 // block_width, block_width)
        result = jnp.einsum("xyzc,ic->xyzi", blocks, tiled_matrix, precision=highest)
    return result.reshape(grid_field.shape)


def face_masks(extent):
    node = lax.iota(jnp.int32, extent) % POLY
    return (node == 0, node == POLY - 1)


def assemble(grid_field):
    extent0, extent1, extent2 = grid_field.shape
    first0, last0 = face_masks(extent0)
    first1, last1 = face_masks(extent1)
    first2, last2 = face_masks(extent2)
    first0, last0 = (first0[:, None, None], last0[:, None, None])
    first1, last1 = (first1[None, :, None], last1[None, :, None])
    first2, last2 = (first2[None, None, :], last2[None, None, :])
    nothing = jnp.zeros_like(grid_field)
    padded = with_halo(grid_field, (("stream", 0),), 1)
    running = (
        grid_field + jnp.where(first0, padded[:-2], nothing) + jnp.where(last0, padded[2:], nothing)
    )
    padded = with_halo(running, (("span", 1),), 1)
    running = (
        running
        + jnp.where(first1, padded[:, :-2], nothing)
        + jnp.where(last1, padded[:, 2:], nothing)
    )
    before = jnp.pad(running, ((0, 0), (0, 0), (1, 0)))[:, :, :-1]
    after = jnp.pad(running, ((0, 0), (0, 0), (0, 1)))[:, :, 1:]
    return running + jnp.where(first2, before, nothing) + jnp.where(last2, after, nothing)


def inverse_multiplicity(extent, offset, whole):
    node = lax.iota(jnp.int32, extent) % POLY
    position = offset + lax.iota(jnp.int32, extent)
    inner_face = (node == 0) & (position > 0) | (node == POLY - 1) & (position < whole - 1)
    return jnp.where(inner_face, 0.5, 1.0).astype(jnp.float32)


def mesh_sum(values):
    axes = ("stream", "span")
    count = lax.axis_size(axes)
    spread = jnp.broadcast_to(values[None], (count,) + values.shape)
    gathered = lax.all_to_all(spread, axes, 0, 0, tiled=True)
    return jnp.sum(gathered, axis=0)


def spread_points(arrived, abscissa, extent0, extent1, extent2):
    elems_y, elems_z = (extent1 // POLY, extent2 // POLY)
    kernels = []
    for dimension in range(3):
        kernels.append(
            jnp.exp(
                -(((abscissa[None, :] - arrived[:, dimension : dimension + 1]) / kernel_width) ** 2)
            )
        )
    element = arrived[:, 6].astype(jnp.int32) - 1
    valid = element >= 0
    elem_x = element // (elems_y * elems_z)
    elem_y = (element // elems_z) % elems_y
    elem_z = element % elems_z
    grid0 = lax.iota(jnp.int32, extent0)
    grid1 = lax.iota(jnp.int32, extent1)
    grid2 = lax.iota(jnp.int32, extent2)
    node0 = jnp.tile(kernels[0], (1, extent0 // POLY))
    node1 = jnp.tile(kernels[1], (1, extent1 // POLY))
    node2 = jnp.tile(kernels[2], (1, extent2 // POLY))
    along0 = jnp.where(elem_x[:, None] == grid0[None, :] // POLY, node0, 0.0)
    along1 = jnp.where(elem_y[:, None] == grid1[None, :] // POLY, node1, 0.0)
    along2 = jnp.where(
        valid[:, None] & (elem_z[:, None] == grid2[None, :] // POLY), node2, 0.0
    )
    left = arrived[:, 3:6][:, :, None, None] * (along0[:, None, :, None] * along1[:, None, None, :])
    return jnp.einsum("pcxy,pz->cxyz", left, along2, precision=lax.Precision.HIGHEST)


def project_points(coords, forces, line_id, line_gain, dest_span, owner_element, abscissa, extents):
    points_dev = coords.shape[1]
    spans = lax.axis_size("span")
    capacity = max(2, 2 * points_dev // spans)
    table_ids = lax.iota(jnp.int32, line_gain.shape[0])
    gains = jnp.sum(
        jnp.where(line_id[:, None] == table_ids[None, :], line_gain[None, :], 0.0), axis=1
    )
    scaled = forces * gains[None, :]
    target = dest_span[:, 0]
    owner_code = (owner_element + 1).astype(jnp.float32)
    payload = jnp.concatenate(
        [coords, scaled, owner_code[None, :], target.astype(jnp.float32)[None, :]], axis=0
    ).T
    order = lax.iota(jnp.int32, points_dev)
    earlier = (target[:, None] == target[None, :]) & (order[None, :] < order[:, None])
    ranks = jnp.sum(earlier.astype(jnp.int32), axis=1)
    slot_at = target * capacity + ranks
    outgoing = jnp.zeros((spans * capacity, 8), jnp.float32).at[slot_at].set(payload)
    outgoing = outgoing.reshape(spans, capacity * 8)
    arrived = lax.all_to_all(outgoing, "span", split_axis=0, concat_axis=0, tiled=True).reshape(
        spans * capacity, 8
    )
    return spread_points(arrived, abscissa, extents[0], extents[1], extents[2])


def local_operator(grid_field, weight3, metric, diffmat):
    running = weight3 * grid_field
    for axis_at in range(3):
        running = running + derive(
            metric * derive(grid_field, diffmat, axis_at, False), diffmat, axis_at, True
        )
    return running


def on_device(velocity, coefficient, coords, forces, line_id, line_gain, dest_span, owner_element):
    abscissa, weights, diffmat = gll_tables()
    extent0, extent1, extent2 = coefficient.shape
    tile_zero = jnp.tile(weights, extent0 // POLY)
    tile_one = jnp.tile(weights, extent1 // POLY)
    tile_two = jnp.tile(weights, extent2 // POLY)
    weight3 = tile_zero[:, None, None] * tile_one[None, :, None] * tile_two[None, None, :]
    metric = weight3 * coefficient
    inv_zero = inverse_multiplicity(
        extent0, lax.axis_index("stream") * extent0, extent0 * lax.axis_size("stream")
    )
    inv_one = inverse_multiplicity(
        extent1, lax.axis_index("span") * extent1, extent1 * lax.axis_size("span")
    )
    inv_two = inverse_multiplicity(extent2, 0, extent2)
    inv_mult = inv_zero[:, None, None] * inv_one[None, :, None] * inv_two[None, None, :]
    forcing = project_points(
        coords,
        forces,
        line_id,
        line_gain,
        dest_span,
        owner_element,
        abscissa,
        (extent0, extent1, extent2),
    )
    running = derive(weight3 * (velocity[0] + forcing[0]), diffmat, 0, True)
    running = running + derive(weight3 * (velocity[1] + forcing[1]), diffmat, 1, True)
    running = running + derive(weight3 * (velocity[2] + forcing[2]), diffmat, 2, True)
    rhs = assemble(running)

    pressure = jnp.zeros_like(rhs)
    residual = rhs
    direction = rhs
    local = local_operator(residual, weight3, metric, diffmat)
    terms = jnp.stack([residual * residual * inv_mult, residual * local])
    sums = mesh_sum(jnp.sum(terms, axis=(1, 2, 3)))
    norm_now, curvature = sums[0], sums[1]
    searched = assemble(local)
    step_len = norm_now / curvature
    for iteration in range(1, ITERS + 1):
        pressure = pressure + step_len * direction
        residual = residual - step_len * searched
        if iteration == ITERS:
            break
        local = local_operator(residual, weight3, metric, diffmat)
        terms = jnp.stack(
            [residual * residual * inv_mult, residual * local, residual * searched * inv_mult]
        )
        sums = mesh_sum(jnp.sum(terms, axis=(1, 2, 3)))
        applied = assemble(local)
        norm_next, own_curvature, cross = sums[0], sums[1], sums[2]
        ratio = norm_next / norm_now
        direction = residual + ratio * direction
        searched = applied + ratio * searched
        curvature = own_curvature + 2.0 * ratio * cross + ratio * ratio * curvature
        norm_now = norm_next
        step_len = norm_now / curvature
    return (pressure, residual)


def solution(mesh):
    return jax.shard_map(
        on_device,
        mesh=mesh,
        in_specs=(
            P(None, "stream", "span", None),
            P("stream", "span", None),
            P(None, ("stream", "span")),
            P(None, ("stream", "span")),
            P(("stream", "span")),
            P(),
            P(("stream", "span"), None),
            P(("stream", "span")),
        ),
        out_specs=(P("stream", "span", None), P("stream", "span", None)),
        check_vma=False,
    )
```

```python
import jax
import jax.numpy as jnp
from jax import lax
from jax.sharding import PartitionSpec as P

POLY = 8
ITERS = 3


kernel_width = 0.45
gll_nodes = [
    -1.0,
    -0.8717401485096066,
    -0.5917001814331423,
    -0.2092992179024789,
    0.2092992179024789,
    0.5917001814331423,
    0.8717401485096066,
    1.0,
]


def with_halo(x, sides, width):
    for axis, dim in sides:
        size, length = (lax.axis_size(axis), x.shape[dim])
        up = [(i, (i + 1) % size) for i in range(size - 1)]
        down = [(j, i) for i, j in up]
        last = lax.slice_in_dim(x, length - width, length, axis=dim)
        first = lax.slice_in_dim(x, 0, width, axis=dim)
        before = lax.ppermute(last, axis, up)
        after = lax.ppermute(first, axis, down)
        x = jnp.concatenate([before, x, after], axis=dim)
    return x


def legendre_value(point, degree):
    previous = 1.0
    current = point
    for order in range(1, degree):
        following = ((2 * order + 1) * point * current - order * previous) / (order + 1)
        previous = current
        current = following
    return current


def gll_tables():
    degree = POLY - 1
    values = [legendre_value(point, degree) for point in gll_nodes]
    weights = [2.0 / (degree * (degree + 1) * value * value) for value in values]
    diffmat = []
    for row_at in range(POLY):
        row_list = []
        for col_at in range(POLY):
            if row_at != col_at:
                row_list.append(
                    values[row_at] / (values[col_at] * (gll_nodes[row_at] - gll_nodes[col_at]))
                )
            elif row_at == 0:
                row_list.append(-degree * (degree + 1) / 4.0)
            elif row_at == degree:
                row_list.append(degree * (degree + 1) / 4.0)
            else:
                row_list.append(0.0)
        diffmat.append(row_list)
    return (
        jnp.asarray(gll_nodes, dtype=jnp.float32),
        jnp.asarray(weights, dtype=jnp.float32),
        jnp.asarray(diffmat, dtype=jnp.float32),
    )


def derive(grid_field, diffmat, axis_at, flipped):
    matrix = diffmat.T if flipped else diffmat
    extent0, extent1, extent2 = grid_field.shape
    highest = lax.Precision.HIGHEST
    if axis_at == 0:
        blocks = grid_field.reshape(extent0 // POLY, POLY, extent1, extent2)
        result = jnp.einsum("ia,xayz->xiyz", matrix, blocks, precision=highest)
    elif axis_at == 1:
        tiled_matrix = jnp.kron(jnp.eye(extent1 // POLY, dtype=jnp.float32), matrix)
        result = jnp.einsum("ib,xbz->xiz", tiled_matrix, grid_field, precision=highest)
    else:
        block_width = 128
        tiled_matrix = jnp.kron(jnp.eye(block_width // POLY, dtype=jnp.float32), matrix)
        blocks = grid_field.reshape(extent0, extent1, extent2 // block_width, block_width)
        result = jnp.einsum("xyzc,ic->xyzi", blocks, tiled_matrix, precision=highest)
    return result.reshape(grid_field.shape)


def face_masks(extent):
    node = lax.iota(jnp.int32, extent) % POLY
    return (node == 0, node == POLY - 1)


def assemble(grid_field):
    extent0, extent1, extent2 = grid_field.shape
    first0, last0 = face_masks(extent0)
    first1, last1 = face_masks(extent1)
    first2, last2 = face_masks(extent2)
    first0, last0 = (first0[:, None, None], last0[:, None, None])
    first1, last1 = (first1[None, :, None], last1[None, :, None])
    first2, last2 = (first2[None, None, :], last2[None, None, :])
    nothing = jnp.zeros_like(grid_field)
    padded = with_halo(grid_field, (("stream", 0),), 1)
    running = (
        grid_field + jnp.where(first0, padded[:-2], nothing) + jnp.where(last0, padded[2:], nothing)
    )
    padded = with_halo(running, (("span", 1),), 1)
    running = (
        running
        + jnp.where(first1, padded[:, :-2], nothing)
        + jnp.where(last1, padded[:, 2:], nothing)
    )
    before = jnp.pad(running, ((0, 0), (0, 0), (1, 0)))[:, :, :-1]
    after = jnp.pad(running, ((0, 0), (0, 0), (0, 1)))[:, :, 1:]
    return running + jnp.where(first2, before, nothing) + jnp.where(last2, after, nothing)


def inverse_multiplicity(extent, offset, whole):
    node = lax.iota(jnp.int32, extent) % POLY
    position = offset + lax.iota(jnp.int32, extent)
    inner_face = (node == 0) & (position > 0) | (node == POLY - 1) & (position < whole - 1)
    return jnp.where(inner_face, 0.5, 1.0).astype(jnp.float32)


def mesh_sum(values):
    axes = ("stream", "span")
    count = lax.axis_size(axes)
    spread = jnp.broadcast_to(values[None], (count,) + values.shape)
    gathered = lax.all_to_all(spread, axes, 0, 0, tiled=True)
    return jnp.sum(gathered, axis=0)[:, None, None, None]


def spread_points(arrived, abscissa, extent0, extent1, extent2):
    elems_y, elems_z = (extent1 // POLY, extent2 // POLY)
    kernels = []
    for dimension in range(3):
        kernels.append(
            jnp.exp(
                -(((abscissa[None, :] - arrived[:, dimension : dimension + 1]) / kernel_width) ** 2)
            )
        )
    element = arrived[:, 6].astype(jnp.int32) - 1
    valid = element >= 0
    elem_x = element // (elems_y * elems_z)
    elem_y = (element // elems_z) % elems_y
    elem_z = element % elems_z
    grid0 = lax.iota(jnp.int32, extent0)
    grid1 = lax.iota(jnp.int32, extent1)
    grid2 = lax.iota(jnp.int32, extent2)
    node0 = jnp.tile(kernels[0], (1, extent0 // POLY))
    node1 = jnp.tile(kernels[1], (1, extent1 // POLY))
    node2 = jnp.tile(kernels[2], (1, extent2 // POLY))
    along0 = jnp.where(elem_x[:, None] == grid0[None, :] // POLY, node0, 0.0)
    along1 = jnp.where(elem_y[:, None] == grid1[None, :] // POLY, node1, 0.0)
    along2 = jnp.where(
        valid[:, None] & (elem_z[:, None] == grid2[None, :] // POLY), node2, 0.0
    )
    left = arrived[:, 3:6][:, :, None, None] * (along0[:, None, :, None] * along1[:, None, None, :])
    return jnp.einsum("pcxy,pz->cxyz", left, along2, precision=lax.Precision.HIGHEST)


def project_points(coords, forces, line_id, line_gain, dest_span, owner_element, abscissa, extents):
    points_dev = coords.shape[1]
    spans = lax.axis_size("span")
    capacity = max(2, 2 * points_dev // spans)
    table_ids = lax.iota(jnp.int32, line_gain.shape[0])
    gains = jnp.sum(
        jnp.where(line_id[:, None] == table_ids[None, :], line_gain[None, :], 0.0), axis=1
    )
    scaled = forces * gains[None, :]
    target = dest_span[:, 0]
    owner_code = (owner_element + 1).astype(jnp.float32)
    payload = jnp.concatenate(
        [coords, scaled, owner_code[None, :], target.astype(jnp.float32)[None, :]], axis=0
    ).T
    order = lax.iota(jnp.int32, points_dev)
    earlier = (target[:, None] == target[None, :]) & (order[None, :] < order[:, None])
    ranks = jnp.sum(earlier.astype(jnp.int32), axis=1)
    slot_at = target * capacity + ranks
    outgoing = jnp.zeros((spans * capacity, 8), jnp.float32).at[slot_at].set(payload)
    outgoing = outgoing.reshape(spans, capacity, 8)
    arrived = lax.all_to_all(outgoing, "span", split_axis=0, concat_axis=0, tiled=True).reshape(
        spans * capacity, 8
    )
    return spread_points(arrived, abscissa, extents[0], extents[1], extents[2])


def local_operator(grid_field, weight3, metric, diffmat):
    running = weight3 * grid_field
    for axis_at in range(3):
        running = running + derive(
            metric * derive(grid_field, diffmat, axis_at, False), diffmat, axis_at, True
        )
    return running


def on_device(velocity, coefficient, coords, forces, line_id, line_gain, dest_span, owner_element):
    abscissa, weights, diffmat = gll_tables()
    extent0, extent1, extent2 = coefficient.shape
    tile_zero = jnp.tile(weights, extent0 // POLY)
    tile_one = jnp.tile(weights, extent1 // POLY)
    tile_two = jnp.tile(weights, extent2 // POLY)
    weight3 = tile_zero[:, None, None] * tile_one[None, :, None] * tile_two[None, None, :]
    metric = weight3 * coefficient
    inv_zero = inverse_multiplicity(
        extent0, lax.axis_index("stream") * extent0, extent0 * lax.axis_size("stream")
    )
    inv_one = inverse_multiplicity(
        extent1, lax.axis_index("span") * extent1, extent1 * lax.axis_size("span")
    )
    inv_two = inverse_multiplicity(extent2, 0, extent2)
    inv_mult = inv_zero[:, None, None] * inv_one[None, :, None] * inv_two[None, None, :]
    forcing = project_points(
        coords,
        forces,
        line_id,
        line_gain,
        dest_span,
        owner_element,
        abscissa,
        (extent0, extent1, extent2),
    )
    running = derive(weight3 * (velocity[0] + forcing[0]), diffmat, 0, True)
    running = running + derive(weight3 * (velocity[1] + forcing[1]), diffmat, 1, True)
    running = running + derive(weight3 * (velocity[2] + forcing[2]), diffmat, 2, True)
    rhs = assemble(running)

    pressure = jnp.zeros_like(rhs)
    residual = rhs
    direction = rhs
    local = local_operator(residual, weight3, metric, diffmat)
    terms = jnp.stack([residual * residual * inv_mult, residual * local])
    sums = mesh_sum(jnp.sum(terms, axis=(1, 2, 3)))
    norm_now, curvature = sums[0], sums[1]
    searched = assemble(local)
    step_len = norm_now / curvature
    for iteration in range(1, ITERS + 1):
        pressure = pressure + step_len * direction
        residual = residual - step_len * searched
        if iteration == ITERS:
            break
        local = local_operator(residual, weight3, metric, diffmat)
        terms = jnp.stack(
            [residual * residual * inv_mult, residual * local, residual * searched * inv_mult]
        )
        sums = mesh_sum(jnp.sum(terms, axis=(1, 2, 3)))
        applied = assemble(local)
        norm_next, own_curvature, cross = sums[0], sums[1], sums[2]
        ratio = norm_next / norm_now
        direction = residual + ratio * direction
        searched = applied + ratio * searched
        curvature = own_curvature + 2.0 * ratio * cross + ratio * ratio * curvature
        norm_now = norm_next
        step_len = norm_now / curvature
    return (pressure, residual)


def solution(mesh):
    return jax.shard_map(
        on_device,
        mesh=mesh,
        in_specs=(
            P(None, "stream", "span", None),
            P("stream", "span", None),
            P(None, ("stream", "span")),
            P(None, ("stream", "span")),
            P(("stream", "span")),
            P(),
            P(("stream", "span"), None),
            P(("stream", "span")),
        ),
        out_specs=(P("stream", "span", None), P("stream", "span", None)),
        check_vma=False,
    )
```
